256 devices in a mesh: gx: 32 (over z, y), gy: 4 (over x), gz: 2 (over core).
Axes of the slice: x: 4, y: 4, z: 8, core: 2. Of those that a mesh axis runs over, the one named last changes fastest.
Arguments:
- volt: float32 [32, 1024, 512], P('gz', 'gx', 'gy'), may hold values from 0 to 1
- recovery: float32 [32, 1024, 512], P('gz', 'gx', 'gy'), may hold values from 0 to 1
- fiber_class: int32 [32, 1024, 512], P('gz', 'gx', 'gy'), may hold values from 0 to 7
- fiber_table: float32 [3, 8], replicated, may hold values from 0.02 to 0.16
- junction_block: int32 [32768], P(('gx', 'gy', 'gz')), may hold values from 0 to 511
- junction_term: int32 [32768], P(('gx', 'gy', 'gz')), may hold values from 0 to 31
- junction_owner: int32 [32768, 1], P(('gx', 'gy', 'gz')), may hold values from 0 to 127; in each aligned block of 128 rows (0 to 127, 128 to 255, ...) at most 2 rows name the same one
- term_volt: float32 [8192, 128], P(('gx', 'gy', 'gz')), may hold values from 0 to 1
- term_recovery: float32 [8192, 128], P(('gx', 'gy', 'gz')), may hold values from 0 to 1
- term_gain: float32 [8192], P(('gx', 'gy', 'gz')), may hold values from 0.5 to 4
- cable_gain: float32 [8192], P(('gx', 'gy', 'gz')), may hold values from 0.05 to 0.45
Outputs:
- volt_out: float32 [32, 1024, 512], P('gz', 'gx', 'gy')
- recovery_out: float32 [32, 1024, 512], P('gz', 'gx', 'gy')
- term_volt_out: float32 [8192, 128], P(('gx', 'gy', 'gz'))
- term_recovery_out: float32 [8192, 128], P(('gx', 'gy', 'gz'))
The draws below stay inside these ranges and needn't reach their ends.
Inputs may be any that keep to these rules, and one draw needn't show every extreme that they name: `junction_owner`: among the 128 junctions of one device, at most 2 have the same owner, a bound that some block reaches.
All inputs are finite; a program needn't handle non-finite values.
Results may differ from the reference program's by a relative error of at most 0.00002.
Values sent between devices are 32-bit elements; how exact they have to be, the bound alone decides.
No kernel may reach another device: no remote copies, remote signals or barrier semaphores. Data moves between devices by JAX's collectives and lax.ppermute only.
A program may use at most 64 MiB of HBM per device.

```python
import math
import jax
import jax.numpy as jnp
import numpy as np

CX = 32
CY = 128
CZ = 16
NCLASS = 8
TERM_DEV = 32
JD = 128
STEPS = 4
CAP = 2
NX = 1024
NY = 512
NZ = 32
JUNCTIONS = 32768
TERMINALS = 8192
N_GX = 32
N_GY = 4
N_GZ = 2


def with_ends(array, key, smallest, largest):
    index_at = [jax.random.randint(jax.random.fold_in(key, axis), (), 0, length) for axis, length in enumerate(array.shape)]
    widest = array.shape.index(max(array.shape))
    neighbour = index_at[:widest] + [(index_at[widest] + 1) % array.shape[widest]] + index_at[widest + 1:]
    return array.at[tuple(index_at)].set(smallest).at[tuple(neighbour)].set(largest)


def block_levels(rng, dims, pieces, smallest, largest):
    def one(position, shards_of):
        draws = jax.random.uniform(jax.random.fold_in(jax.random.fold_in(rng, 6), position), (shards_of,), jnp.float32, smallest / len(pieces), largest / len(pieces))
        return jnp.repeat(jnp.exp(draws), dims[position] // shards_of).reshape((-1,) + (1,) * (len(dims) - position - 1))

    loudness = one(*pieces[0])
    for cut in pieces[1:]:
        loudness = loudness * one(*cut)
    return loudness


def assign_block(own_key, own, number, rows, amount, top, most, skew):
    sequence = jax.random.permutation(own_key, amount)
    heavy_load, common = shares(amount, rows * top, most, skew, True), shares(amount, rows * top, most, skew, False)
    places = jnp.arange(amount)

    def named(sizes, rotation):
        used = int((sizes > 0).sum())
        fixed = max(1, used // 4)
        moved = fixed + (places - fixed + rotation * (used - fixed)) % max(1, amount - fixed)
        return jnp.zeros((amount,), jnp.int32).at[sequence[jnp.where(places < fixed, places, moved)]].set(jnp.asarray(sizes, jnp.int32))

    sizes = jnp.where(number % 4 == 0, named(heavy_load, number // 4), named(common, number - number // 4 - 1))
    mixed = jax.random.permutation(jax.random.fold_in(own, 3), amount)
    donor, sink = mixed[0:amount // 2 * 2:2], mixed[1:amount // 2 * 2:2]
    margin = jnp.minimum(sizes[donor] - 1, most - sizes[sink]) // 2
    margin = jnp.where((donor == sequence[0]) | (sink == sequence[0]) | (sizes[sink] == 0), 0, jnp.maximum(margin, 0))
    moved = jax.random.randint(jax.random.fold_in(own, 4), (amount // 2,), 0, 1 << 20) % (margin + 1)
    sizes = sizes.at[donor].add(-moved).at[sink].add(moved)
    members = jnp.searchsorted(jnp.cumsum(sizes), jnp.arange(rows * top), side="right").astype(jnp.int32)
    table = members.reshape(top, rows).T
    table = table[jax.random.permutation(jax.random.fold_in(own, 1), rows)]
    rotation = jax.random.randint(jax.random.fold_in(own, 2), (rows, 1), 0, top)
    return jnp.take_along_axis(table, (jnp.arange(top)[None, :] + rotation) % top, axis=1)


def shares(count, total, reach, skew, full):
    loads = [(1 << 20) // math.isqrt(rank ** skew) + 1 for rank in range(1, count + 1)]
    largest = reach if full else min(reach, max(-(-total // count), total * loads[0] // sum(loads)))
    least = 1 if total - largest >= count - 1 else 0
    counts, rest = [largest] + [least] * (count - 1), total - largest - least * (count - 1)
    while rest > 0:
        candidates = [i for i in range(1, count) if counts[i] < largest] or [i for i in range(1, count) if counts[i] < reach]
        pool, budget = sum([loads[i] for i in candidates]), rest
        for i in candidates:
            more = min(reach - counts[i], max(1, budget * loads[i] // pool), rest)
            counts[i] = counts[i] + more
            rest = rest - more
    return np.array(counts)


def setup_inputs(seed: int = 0) -> dict:
    splits = jax.random.split(jax.random.key(seed), 12)
    volt = jnp.clip(1.0 * jax.random.uniform(splits[0], (NZ, NX, NY), jnp.float32) ** block_levels(splits[0], (NZ, NX, NY), ((0, 2), (1, 32), (2, 4)), -0.2, 0.2), 0.0, 1.0)
    recovery = jnp.clip(1.0 * jax.random.uniform(splits[1], (NZ, NX, NY), jnp.float32) ** block_levels(splits[1], (NZ, NX, NY), ((0, 2), (1, 32), (2, 4)), -0.2, 0.2), 0.0, 1.0)
    fiber_class = with_ends(jax.random.randint(splits[2], (NZ, NX, NY), 0, NCLASS), jax.random.fold_in(splits[2], 1), 0, NCLASS - 1).astype(jnp.int32)
    fiber_table = jnp.clip(jax.random.uniform(splits[3], (3, NCLASS), jnp.float32, 0.02, 0.16), 0.02, 0.16)
    junction_block = with_ends(jax.random.randint(splits[4], (JUNCTIONS,), 0, CZ * CX), jax.random.fold_in(splits[4], 1), 0, (CZ * CX) - 1).astype(jnp.int32)
    junction_term = with_ends(jax.random.randint(splits[5], (JUNCTIONS,), 0, TERM_DEV), jax.random.fold_in(splits[5], 1), 0, TERM_DEV - 1).astype(jnp.int32)
    junction_owner_keys = jax.random.split(jax.random.fold_in(splits[6], 1), JUNCTIONS // JD)
    junction_owner_turns = jax.random.permutation(jax.random.fold_in(splits[6], 3), JUNCTIONS // JD)
    junction_owner = jax.vmap(lambda own, number: assign_block(jax.random.fold_in(splits[6], 2), own, number, JD, N_GX * N_GY, 1, CAP, 2))(junction_owner_keys, junction_owner_turns).reshape((JUNCTIONS, 1))
    term_volt = jnp.clip(1.0 * jax.random.uniform(splits[7], (TERMINALS, CY), jnp.float32) ** block_levels(splits[7], (TERMINALS, CY), ((0, 256),), -0.2, 0.2), 0.0, 1.0)
    term_recovery = jnp.clip(1.0 * jax.random.uniform(splits[8], (TERMINALS, CY), jnp.float32) ** block_levels(splits[8], (TERMINALS, CY), ((0, 256),), -0.2, 0.2), 0.0, 1.0)
    term_gain = jnp.clip(jnp.exp(math.log(4.0) - 2.0794415 * jax.random.uniform(splits[9], (TERMINALS,), jnp.float32) ** block_levels(splits[9], (TERMINALS,), ((0, 256),), -0.2, 0.2)), 0.5, 4.0)
    cable_gain = jnp.clip(jnp.exp(math.log(0.45) - 2.1972245 * jax.random.uniform(splits[10], (TERMINALS,), jnp.float32) ** block_levels(splits[10], (TERMINALS,), ((0, 256),), -0.2, 0.2)), 0.05, 0.45)
    return dict(volt=volt, recovery=recovery, fiber_class=fiber_class, fiber_table=fiber_table, junction_block=junction_block, junction_term=junction_term, junction_owner=junction_owner, term_volt=term_volt, term_recovery=term_recovery, term_gain=term_gain, cable_gain=cable_gain)


def cell_kinetics(v, w, drive):
    react = -8.0 * v * (v - 0.15) * (v - 1.0) - v * w
    new_v = 0.1 * (react + drive)
    new_w = w + 0.01 * (-w - 8.0 * v * (v - 1.15))
    return new_v, new_w


def reference(volt, recovery, fiber_class, fiber_table, junction_block, junction_term, junction_owner, term_volt, term_recovery, term_gain, cable_gain):
    coef_z = jnp.zeros(volt.shape, jnp.float32)
    coef_x = jnp.zeros(volt.shape, jnp.float32)
    coef_y = jnp.zeros(volt.shape, jnp.float32)
    for klass in range(NCLASS):
        hit = fiber_class == klass
        coef_z = jnp.where(hit, fiber_table[0, klass], coef_z)
        coef_x = jnp.where(hit, fiber_table[1, klass], coef_x)
        coef_y = jnp.where(hit, fiber_table[2, klass], coef_y)
    index = jnp.arange(JUNCTIONS, dtype=jnp.int32)
    block_dev = index // JD
    tile_x = block_dev // (N_GY * N_GZ)
    tile_y = (block_dev // N_GZ) % N_GY
    tile_z = block_dev % N_GZ
    depth_at = tile_z * CZ + junction_block // CX
    row_at = tile_x * CX + junction_block % CX
    target = (junction_owner[:, 0] * N_GZ + tile_z) * TERM_DEV + junction_term
    gains = term_gain[target]
    for step in range(STEPS):
        grid = volt.reshape(NZ, NX, N_GY, CY)
        rows = grid[depth_at, row_at, tile_y]
        current = gains[:, None] * (term_volt[target] - rows)
        into_voxel = jnp.zeros((NZ, NX, N_GY, CY), jnp.float32).at[depth_at, row_at, tile_y].add(current).reshape(NZ, NX, NY)
        into_term = jnp.zeros((TERMINALS, CY), jnp.float32).at[target].add(-current)
        padded = jnp.pad(volt, 1, mode="edge")
        lap_z = (padded[2:, 1:-1, 1:-1] + padded[:-2, 1:-1, 1:-1]) - 2.0 * volt
        lap_x = (padded[1:-1, 2:, 1:-1] + padded[1:-1, :-2, 1:-1]) - 2.0 * volt
        lap_y = (padded[1:-1, 1:-1, 2:] + padded[1:-1, 1:-1, :-2]) - 2.0 * volt
        react_v, new_w = cell_kinetics(volt, recovery, into_voxel)
        new_v = volt + (coef_z * lap_z + coef_x * lap_x + coef_y * lap_y) + react_v
        cable = jnp.pad(term_volt, ((0, 0), (1, 1)), mode="edge")
        lap_k = (cable[:, 2:] + cable[:, :-2]) - 2.0 * term_volt
        react_u, new_r = cell_kinetics(term_volt, term_recovery, 0.1 * into_term)
        new_u = term_volt + cable_gain[:, None] * lap_k + react_u
        volt, recovery, term_volt, term_recovery = new_v, new_w, new_u, new_r
    return volt, recovery, term_volt, term_recovery
```

```python
import jax
import jax.numpy as jnp
from jax import lax
from jax.sharding import PartitionSpec as P

NCLASS = 8
STEPS = 4


def cell_kinetics(v, w, drive):
    react = -8.0 * v * (v - 0.15) * (v - 1.0) - v * w
    new_v = 0.1 * (react + drive)
    new_w = w + 0.01 * (-w - 8.0 * v * (v - 1.15))
    return (new_v, new_w)


def neighbours(cells, axis, dim):
    count = lax.axis_size(axis)
    index = lax.axis_index(axis)
    size = cells.shape[dim]
    first = lax.slice_in_dim(cells, 0, 1, axis=dim)
    last = lax.slice_in_dim(cells, size - 1, size, axis=dim)
    from_low = lax.ppermute(last, axis, [(i, i + 1) for i in range(count - 1)])
    from_high = lax.ppermute(first, axis, [(i + 1, i) for i in range(count - 1)])
    low = jnp.where(index == 0, first, from_low)
    high = jnp.where(index == count - 1, last, from_high)
    plus = jnp.concatenate([lax.slice_in_dim(cells, 1, size, axis=dim), high], axis=dim)
    minus = jnp.concatenate([low, lax.slice_in_dim(cells, 0, size - 1, axis=dim)], axis=dim)
    return plus, minus


def on_device(
    volt,
    recovery,
    fiber_class,
    fiber_table,
    junction_block,
    junction_term,
    junction_owner,
    term_volt,
    term_recovery,
    term_gain,
    cable_gain,
):
    depth, rows_x, width = volt.shape
    owners = lax.axis_size("gx") * lax.axis_size("gy")
    jcount = junction_block.shape[0]
    capacity = max(2, 2 * jcount // owners)
    slots_total = owners * capacity
    term_count = term_volt.shape[0]
    coef_z = jnp.zeros(volt.shape, jnp.float32)
    coef_x = jnp.zeros(volt.shape, jnp.float32)
    coef_y = jnp.zeros(volt.shape, jnp.float32)
    for klass in range(NCLASS):
        hit = fiber_class == klass
        coef_z = jnp.where(hit, fiber_table[0, klass], coef_z)
        coef_x = jnp.where(hit, fiber_table[1, klass], coef_x)
        coef_y = jnp.where(hit, fiber_table[2, klass], coef_y)
    coef_z, coef_x, coef_y = lax.optimization_barrier((coef_z, coef_x, coef_y))

    owner = junction_owner[:, 0]
    order = jnp.arange(jcount, dtype=jnp.int32)
    earlier = (owner[:, None] == owner[None, :]) & (order[None, :] < order[:, None])
    rank = jnp.sum(earlier.astype(jnp.int32), axis=1)
    slot = owner * capacity + rank
    hits = slot[None, :] == jnp.arange(slots_total, dtype=jnp.int32)[:, None]
    slot_used = jnp.any(hits, axis=1)
    slot_block = jnp.sum(jnp.where(hits, junction_block[None, :], 0), axis=1)
    slot_term = jnp.sum(jnp.where(hits, junction_term[None, :] + 1, 0), axis=1) - 1

    arrived = lax.all_to_all(slot_term, ("gx", "gy"), split_axis=0, concat_axis=0, tiled=True)
    valid = arrived >= 0
    safe_ids = jnp.where(valid, arrived, 0)
    pick = safe_ids[:, None] == jnp.arange(term_count, dtype=jnp.int32)[None, :]
    gains = jnp.where(valid, jnp.sum(jnp.where(pick, term_gain[None, :], 0.0), axis=1), 0.0)
    gain_rows = jnp.broadcast_to(gains[:, None], (slots_total, width))

    tile_gain = None
    for step in range(STEPS):
        flat_rows = volt.reshape(depth * rows_x, width)
        rows = flat_rows[junction_block]
        out_rows = jnp.where(slot_used[:, None], flat_rows[slot_block], 0.0)
        far_volt = term_volt[safe_ids]
        parts = [out_rows, far_volt] + ([gain_rows] if step == 0 else [])
        sent = jnp.stack(parts, axis=1)
        received = lax.all_to_all(sent, ("gx", "gy"), split_axis=0, concat_axis=0, tiled=True)
        current = gains[:, None] * (far_volt - received[:, 0, :])
        into_term = jax.ops.segment_sum(-current, safe_ids, num_segments=term_count)
        mine = received[slot]
        if step == 0:
            tile_gain = mine[:, 2, :]
        tile_current = tile_gain * (mine[:, 1, :] - rows)
        into_voxel = jax.ops.segment_sum(
            tile_current, junction_block, num_segments=depth * rows_x
        ).reshape(depth, rows_x, width)
        z_plus, z_minus = neighbours(volt, "gz", 0)
        x_plus, x_minus = neighbours(volt, "gx", 1)
        y_plus, y_minus = neighbours(volt, "gy", 2)
        lap_z = z_plus + z_minus - 2.0 * volt
        lap_x = x_plus + x_minus - 2.0 * volt
        lap_y = y_plus + y_minus - 2.0 * volt
        react_v, new_w = cell_kinetics(volt, recovery, into_voxel)
        new_v = volt + (coef_z * lap_z + coef_x * lap_x + coef_y * lap_y) + react_v
        cable = jnp.pad(term_volt, ((0, 0), (1, 1)), mode="edge")
        lap_k = cable[:, 2:] + cable[:, :-2] - 2.0 * term_volt
        react_u, new_r = cell_kinetics(term_volt, term_recovery, 0.1 * into_term)
        new_u = term_volt + cable_gain[:, None] * lap_k + react_u
        volt, recovery, term_volt, term_recovery = (new_v, new_w, new_u, new_r)
    return (volt, recovery, term_volt, term_recovery)


def solution(mesh):
    return jax.shard_map(
        on_device,
        mesh=mesh,
        in_specs=(
            P("gz", "gx", "gy"),
            P("gz", "gx", "gy"),
            P("gz", "gx", "gy"),
            P(),
            P(("gx", "gy", "gz")),
            P(("gx", "gy", "gz")),
            P(("gx", "gy", "gz"), None),
            P(("gx", "gy", "gz"), None),
            P(("gx", "gy", "gz"), None),
            P(("gx", "gy", "gz")),
            P(("gx", "gy", "gz")),
        ),
        out_specs=(
            P("gz", "gx", "gy"),
            P("gz", "gx", "gy"),
            P(("gx", "gy", "gz"), None),
            P(("gx", "gy", "gz"), None),
        ),
        check_vma=False,
    )
```

```python
import jax
import jax.numpy as jnp
from jax import lax
from jax.sharding import PartitionSpec as P

NCLASS = 8
STEPS = 4


def cell_kinetics(v, w, drive):
    react = -8.0 * v * (v - 0.15) * (v - 1.0) - v * w
    new_v = 0.1 * (react + drive)
    new_w = w + 0.01 * (-w - 8.0 * v * (v - 1.15))
    return (new_v, new_w)


def neighbours(cells, axis, dim):
    count = lax.axis_size(axis)
    index = lax.axis_index(axis)
    size = cells.shape[dim]
    first = lax.slice_in_dim(cells, 0, 1, axis=dim)
    last = lax.slice_in_dim(cells, size - 1, size, axis=dim)
    face = first.shape
    if dim == cells.ndim - 1:
        first, last = (x.reshape(-1, 128) for x in (first, last))
    from_low = lax.ppermute(last, axis, [(i, i + 1) for i in range(count - 1)])
    from_high = lax.ppermute(first, axis, [(i + 1, i) for i in range(count - 1)])
    first, last, from_low, from_high = (x.reshape(face) for x in (first, last, from_low, from_high))
    low = jnp.where(index == 0, first, from_low)
    high = jnp.where(index == count - 1, last, from_high)
    plus = jnp.concatenate([lax.slice_in_dim(cells, 1, size, axis=dim), high], axis=dim)
    minus = jnp.concatenate([low, lax.slice_in_dim(cells, 0, size - 1, axis=dim)], axis=dim)
    return plus, minus


def on_device(
    volt,
    recovery,
    fiber_class,
    fiber_table,
    junction_block,
    junction_term,
    junction_owner,
    term_volt,
    term_recovery,
    term_gain,
    cable_gain,
):
    depth, rows_x, width = volt.shape
    owners = lax.axis_size("gx") * lax.axis_size("gy")
    jcount = junction_block.shape[0]
    capacity = max(2, 2 * jcount // owners)
    slots_total = owners * capacity
    term_count = term_volt.shape[0]
    coef_z = jnp.zeros(volt.shape, jnp.float32)
    coef_x = jnp.zeros(volt.shape, jnp.float32)
    coef_y = jnp.zeros(volt.shape, jnp.float32)
    for klass in range(NCLASS):
        hit = fiber_class == klass
        coef_z = jnp.where(hit, fiber_table[0, klass], coef_z)
        coef_x = jnp.where(hit, fiber_table[1, klass], coef_x)
        coef_y = jnp.where(hit, fiber_table[2, klass], coef_y)
    coef_z, coef_x, coef_y = lax.optimization_barrier((coef_z, coef_x, coef_y))

    owner = junction_owner[:, 0]
    order = jnp.arange(jcount, dtype=jnp.int32)
    earlier = (owner[:, None] == owner[None, :]) & (order[None, :] < order[:, None])
    rank = jnp.sum(earlier.astype(jnp.int32), axis=1)
    slot = owner * capacity + rank
    hits = slot[None, :] == jnp.arange(slots_total, dtype=jnp.int32)[:, None]
    slot_used = jnp.any(hits, axis=1)
    slot_block = jnp.sum(jnp.where(hits, junction_block[None, :], 0), axis=1)
    slot_term = jnp.sum(jnp.where(hits, junction_term[None, :] + 1, 0), axis=1) - 1

    arrived = lax.all_to_all(slot_term, ("gx", "gy"), split_axis=0, concat_axis=0, tiled=True)
    valid = arrived >= 0
    safe_ids = jnp.where(valid, arrived, 0)
    pick = safe_ids[:, None] == jnp.arange(term_count, dtype=jnp.int32)[None, :]
    gains = jnp.where(valid, jnp.sum(jnp.where(pick, term_gain[None, :], 0.0), axis=1), 0.0)
    gain_rows = jnp.broadcast_to(gains[:, None], (slots_total, width))

    tile_gain = None
    for step in range(STEPS):
        flat_rows = volt.reshape(depth * rows_x, width)
        rows = flat_rows[junction_block]
        out_rows = jnp.where(slot_used[:, None], flat_rows[slot_block], 0.0)
        far_volt = term_volt[safe_ids]
        parts = [out_rows, far_volt] + ([gain_rows] if step == 0 else [])
        sent = jnp.stack(parts, axis=1)
        received = lax.all_to_all(sent, ("gx", "gy"), split_axis=0, concat_axis=0, tiled=True)
        current = gains[:, None] * (far_volt - received[:, 0, :])
        into_term = jax.ops.segment_sum(-current, safe_ids, num_segments=term_count)
        mine = received[slot]
        if step == 0:
            tile_gain = mine[:, 2, :]
        tile_current = tile_gain * (mine[:, 1, :] - rows)
        into_voxel = jax.ops.segment_sum(
            tile_current, junction_block, num_segments=depth * rows_x
        ).reshape(depth, rows_x, width)
        z_plus, z_minus = neighbours(volt, "gz", 0)
        x_plus, x_minus = neighbours(volt, "gx", 1)
        y_plus, y_minus = neighbours(volt, "gy", 2)
        lap_z = z_plus + z_minus - 2.0 * volt
        lap_x = x_plus + x_minus - 2.0 * volt
        lap_y = y_plus + y_minus - 2.0 * volt
        react_v, new_w = cell_kinetics(volt, recovery, into_voxel)
        new_v = volt + (coef_z * lap_z + coef_x * lap_x + coef_y * lap_y) + react_v
        cable = jnp.pad(term_volt, ((0, 0), (1, 1)), mode="edge")
        lap_k = cable[:, 2:] + cable[:, :-2] - 2.0 * term_volt
        react_u, new_r = cell_kinetics(term_volt, term_recovery, 0.1 * into_term)
        new_u = term_volt + cable_gain[:, None] * lap_k + react_u
        volt, recovery, term_volt, term_recovery = (new_v, new_w, new_u, new_r)
    return (volt, recovery, term_volt, term_recovery)


def solution(mesh):
    return jax.shard_map(
        on_device,
        mesh=mesh,
        in_specs=(
            P("gz", "gx", "gy"),
            P("gz", "gx", "gy"),
            P("gz", "gx", "gy"),
            P(),
            P(("gx", "gy", "gz")),
            P(("gx", "gy", "gz")),
            P(("gx", "gy", "gz"), None),
            P(("gx", "gy", "gz"), None),
            P(("gx", "gy", "gz"), None),
            P(("gx", "gy", "gz")),
            P(("gx", "gy", "gz")),
        ),
        out_specs=(
            P("gz", "gx", "gy"),
            P("gz", "gx", "gy"),
            P(("gx", "gy", "gz"), None),
            P(("gx", "gy", "gz"), None),
        ),
        check_vma=False,
    )
```

```python
import jax
import jax.numpy as jnp
from jax import lax
from jax.sharding import PartitionSpec as P

NCLASS = 8
STEPS = 4


def cell_kinetics(v, w, drive):
    react = -8.0 * v * (v - 0.15) * (v - 1.0) - v * w
    new_v = 0.1 * (react + drive)
    new_w = w + 0.01 * (-w - 8.0 * v * (v - 1.15))
    return (new_v, new_w)


def neighbours(cells, axis, dim):
    count = lax.axis_size(axis)
    index = lax.axis_index(axis)
    size = cells.shape[dim]
    first = lax.slice_in_dim(cells, 0, 1, axis=dim)
    last = lax.slice_in_dim(cells, size - 1, size, axis=dim)
    face = first.shape
    if dim == cells.ndim - 1:
        first, last = (x.reshape(-1, 128) for x in (first, last))
    if count == 2:
        swapped = lax.ppermute(jnp.where(index == 0, last, first), axis, [(0, 1), (1, 0)])
        from_low, from_high = swapped, swapped
    else:
        from_low = lax.ppermute(last, axis, [(i, i + 1) for i in range(count - 1)])
        from_high = lax.ppermute(first, axis, [(i + 1, i) for i in range(count - 1)])
    first, last, from_low, from_high = (x.reshape(face) for x in (first, last, from_low, from_high))
    low = jnp.where(index == 0, first, from_low)
    high = jnp.where(index == count - 1, last, from_high)
    plus = jnp.concatenate([lax.slice_in_dim(cells, 1, size, axis=dim), high], axis=dim)
    minus = jnp.concatenate([low, lax.slice_in_dim(cells, 0, size - 1, axis=dim)], axis=dim)
    return plus, minus


def on_device(
    volt,
    recovery,
    fiber_class,
    fiber_table,
    junction_block,
    junction_term,
    junction_owner,
    term_volt,
    term_recovery,
    term_gain,
    cable_gain,
):
    depth, rows_x, width = volt.shape
    owners = lax.axis_size("gx") * lax.axis_size("gy")
    jcount = junction_block.shape[0]
    capacity = max(2, 2 * jcount // owners)
    slots_total = owners * capacity
    term_count = term_volt.shape[0]
    coef_z = jnp.zeros(volt.shape, jnp.float32)
    coef_x = jnp.zeros(volt.shape, jnp.float32)
    coef_y = jnp.zeros(volt.shape, jnp.float32)
    for klass in range(NCLASS):
        hit = fiber_class == klass
        coef_z = jnp.where(hit, fiber_table[0, klass], coef_z)
        coef_x = jnp.where(hit, fiber_table[1, klass], coef_x)
        coef_y = jnp.where(hit, fiber_table[2, klass], coef_y)
    coef_z, coef_x, coef_y = lax.optimization_barrier((coef_z, coef_x, coef_y))

    owner = junction_owner[:, 0]
    order = jnp.arange(jcount, dtype=jnp.int32)
    earlier = (owner[:, None] == owner[None, :]) & (order[None, :] < order[:, None])
    rank = jnp.sum(earlier.astype(jnp.int32), axis=1)
    slot = owner * capacity + rank
    hits = slot[None, :] == jnp.arange(slots_total, dtype=jnp.int32)[:, None]
    slot_used = jnp.any(hits, axis=1)
    slot_block = jnp.sum(jnp.where(hits, junction_block[None, :], 0), axis=1)
    slot_term = jnp.sum(jnp.where(hits, junction_term[None, :] + 1, 0), axis=1) - 1

    arrived = lax.all_to_all(slot_term, ("gx", "gy"), split_axis=0, concat_axis=0, tiled=True)
    valid = arrived >= 0
    safe_ids = jnp.where(valid, arrived, 0)
    pick = safe_ids[:, None] == jnp.arange(term_count, dtype=jnp.int32)[None, :]
    gains = jnp.where(valid, jnp.sum(jnp.where(pick, term_gain[None, :], 0.0), axis=1), 0.0)
    gain_rows = jnp.broadcast_to(gains[:, None], (slots_total, width))

    tile_gain = None
    for step in range(STEPS):
        flat_rows = volt.reshape(depth * rows_x, width)
        rows = flat_rows[junction_block]
        out_rows = jnp.where(slot_used[:, None], flat_rows[slot_block], 0.0)
        far_volt = term_volt[safe_ids]
        parts = [out_rows, far_volt] + ([gain_rows] if step == 0 else [])
        sent = jnp.stack(parts, axis=1)
        received = lax.all_to_all(sent, ("gx", "gy"), split_axis=0, concat_axis=0, tiled=True)
        current = gains[:, None] * (far_volt - received[:, 0, :])
        into_term = jax.ops.segment_sum(-current, safe_ids, num_segments=term_count)
        mine = received[slot]
        if step == 0:
            tile_gain = mine[:, 2, :]
        tile_current = tile_gain * (mine[:, 1, :] - rows)
        into_voxel = jax.ops.segment_sum(
            tile_current, junction_block, num_segments=depth * rows_x
        ).reshape(depth, rows_x, width)
        z_plus, z_minus = neighbours(volt, "gz", 0)
        x_plus, x_minus = neighbours(volt, "gx", 1)
        y_plus, y_minus = neighbours(volt, "gy", 2)
        lap_z = z_plus + z_minus - 2.0 * volt
        lap_x = x_plus + x_minus - 2.0 * volt
        lap_y = y_plus + y_minus - 2.0 * volt
        react_v, new_w = cell_kinetics(volt, recovery, into_voxel)
        new_v = volt + (coef_z * lap_z + coef_x * lap_x + coef_y * lap_y) + react_v
        cable = jnp.pad(term_volt, ((0, 0), (1, 1)), mode="edge")
        lap_k = cable[:, 2:] + cable[:, :-2] - 2.0 * term_volt
        react_u, new_r = cell_kinetics(term_volt, term_recovery, 0.1 * into_term)
        new_u = term_volt + cable_gain[:, None] * lap_k + react_u
        volt, recovery, term_volt, term_recovery = (new_v, new_w, new_u, new_r)
    return (volt, recovery, term_volt, term_recovery)


def solution(mesh):
    return jax.shard_map(
        on_device,
        mesh=mesh,
        in_specs=(
            P("gz", "gx", "gy"),
            P("gz", "gx", "gy"),
            P("gz", "gx", "gy"),
            P(),
            P(("gx", "gy", "gz")),
            P(("gx", "gy", "gz")),
            P(("gx", "gy", "gz"), None),
            P(("gx", "gy", "gz"), None),
            P(("gx", "gy", "gz"), None),
            P(("gx", "gy", "gz")),
            P(("gx", "gy", "gz")),
        ),
        out_specs=(
            P("gz", "gx", "gy"),
            P("gz", "gx", "gy"),
            P(("gx", "gy", "gz"), None),
            P(("gx", "gy", "gz"), None),
        ),
        check_vma=False,
    )
```

```python
import jax
import jax.numpy as jnp
from jax import lax
from jax.experimental import pallas as pl
from jax.experimental.pallas import tpu as pltpu
from jax.sharding import PartitionSpec as P

NCLASS = 8
STEPS = 4
INTERPRET = False


def cell_kinetics(v, w, drive):
    react = -8.0 * v * (v - 0.15) * (v - 1.0) - v * w
    new_v = 0.1 * (react + drive)
    new_w = w + 0.01 * (-w - 8.0 * v * (v - 1.15))
    return (new_v, new_w)


def shifted(cells, axis):
    size = cells.shape[axis]
    a = pltpu.roll(cells, 1, axis)
    b = pltpu.roll(cells, size - 1, axis)
    pos = lax.broadcasted_iota(jnp.int32, cells.shape, axis)
    moved = pltpu.roll(pos, 1, axis)
    forward = moved == jnp.where(pos == 0, size - 1, pos - 1)
    return jnp.where(forward, a, b), jnp.where(forward, b, a)


def flag(ref, i, shape):
    return jnp.full(shape, ref[i], jnp.int32) > 0


def step_kernel(
    blk_ref, slot_ref, ids_ref, sblk_ref, edge_ref,
    v_ref, w_ref, cz_ref, cx_ref, cy_ref, recv_ref, tg_ref, g_ref,
    tv_ref, tr_ref, cg_ref, zr_ref, xlo_ref, xhi_ref, ylo_ref, yhi_ref,
    nv_ref, nw_ref, ntv_ref, ntr_ref, snd_ref, zs_ref, xf_ref, xl_ref, yf_ref, yl_ref,
    iv_ref, it_ref,
):
    depth, rows_x, width = v_ref.shape
    jcount = blk_ref.shape[0]
    slots = ids_ref.shape[0]
    iv_ref[...] = jnp.zeros(iv_ref.shape, jnp.float32)
    it_ref[...] = jnp.zeros(it_ref.shape, jnp.float32)

    def tile_body(j, carry):
        b = blk_ref[j]
        s = slot_ref[j]
        z = b // rows_x
        x = b % rows_x
        row = v_ref[z, pl.ds(x, 1), :]
        far = recv_ref[pl.ds(s, 1), :][:, width:2 * width]
        cur = tg_ref[pl.ds(j, 1), :] * (far - row)
        iv_ref[z, pl.ds(x, 1), :] = iv_ref[z, pl.ds(x, 1), :] + cur
        return carry

    lax.fori_loop(0, jcount, tile_body, 0)

    def owner_body(k, carry):
        t = ids_ref[k]
        cur = g_ref[pl.ds(k, 1), :] * (tv_ref[pl.ds(t, 1), :] - recv_ref[pl.ds(k, 1), :][:, 0:width])
        it_ref[pl.ds(t, 1), :] = it_ref[pl.ds(t, 1), :] + (-cur)
        return carry

    lax.fori_loop(0, slots, owner_body, 0)

    u = tv_ref[...]
    r = tr_ref[...]
    u_minus, u_plus = shifted(u, 1)
    lane_t = lax.broadcasted_iota(jnp.int32, u.shape, 1)
    u_minus = jnp.where(lane_t == 0, u, u_minus)
    u_plus = jnp.where(lane_t == width - 1, u, u_plus)
    lap_k = u_plus + u_minus - 2.0 * u
    react_u, new_r = cell_kinetics(u, r, 0.1 * it_ref[...])
    ntv_ref[...] = u + cg_ref[...] * lap_k + react_u
    ntr_ref[...] = new_r

    plane = (rows_x, width)
    sub = lax.broadcasted_iota(jnp.int32, plane, 0)
    lane = lax.broadcasted_iota(jnp.int32, plane, 1)
    z_low = flag(edge_ref, 0, plane)
    z_high = flag(edge_ref, 1, plane)
    x_low = flag(edge_ref, 2, (1, width))
    x_high = flag(edge_ref, 3, (1, width))
    y_low = flag(edge_ref, 4, (rows_x, 1))
    y_high = flag(edge_ref, 5, (rows_x, 1))
    per_row = width // rows_x
    y_first = [jnp.zeros((1, width), jnp.float32) for _ in range(yf_ref.shape[0])]
    y_last = [jnp.zeros((1, width), jnp.float32) for _ in range(yf_ref.shape[0])]
    for z in range(depth):
        vz = v_ref[z]
        if z == 0:
            zm = jnp.where(z_low, vz, zr_ref[...])
        else:
            zm = v_ref[z - 1]
        if z == depth - 1:
            zp = jnp.where(z_high, vz, zr_ref[...])
        else:
            zp = v_ref[z + 1]
        xm, xp = shifted(vz, 0)
        x_lo_row = jnp.where(x_low, vz[0:1, :], xlo_ref[z:z + 1, :])
        x_hi_row = jnp.where(x_high, vz[rows_x - 1:rows_x, :], xhi_ref[z:z + 1, :])
        xm = jnp.where(sub == 0, x_lo_row, xm)
        xp = jnp.where(sub == rows_x - 1, x_hi_row, xp)
        ym, yp = shifted(vz, 1)
        row_at, lane_at = z // per_row, (z % per_row) * rows_x
        pick = lane == sub + lane_at
        y_lo_col = jnp.sum(jnp.where(pick, ylo_ref[row_at:row_at + 1, :], 0.0), axis=1, keepdims=True)
        y_hi_col = jnp.sum(jnp.where(pick, yhi_ref[row_at:row_at + 1, :], 0.0), axis=1, keepdims=True)
        y_lo_col = jnp.where(y_low, vz[:, 0:1], y_lo_col)
        y_hi_col = jnp.where(y_high, vz[:, width - 1:width], y_hi_col)
        ym = jnp.where(lane == 0, y_lo_col, ym)
        yp = jnp.where(lane == width - 1, y_hi_col, yp)
        lap_z = zp + zm - 2.0 * vz
        lap_x = xp + xm - 2.0 * vz
        lap_y = yp + ym - 2.0 * vz
        react_v, new_w = cell_kinetics(vz, w_ref[z], iv_ref[z])
        nv = vz + (cz_ref[z] * lap_z + cx_ref[z] * lap_x + cy_ref[z] * lap_y) + react_v
        nv_ref[z] = nv
        nw_ref[z] = new_w
        xf_ref[z:z + 1, :] = nv[0:1, :]
        xl_ref[z:z + 1, :] = nv[rows_x - 1:rows_x, :]
        y_first[row_at] = y_first[row_at] + jnp.sum(
            jnp.where(pick, nv[:, 0:1], 0.0), axis=0, keepdims=True)
        y_last[row_at] = y_last[row_at] + jnp.sum(
            jnp.where(pick, nv[:, width - 1:width], 0.0), axis=0, keepdims=True)
    for i in range(yf_ref.shape[0]):
        yf_ref[i:i + 1, :] = y_first[i]
        yl_ref[i:i + 1, :] = y_last[i]
    zs_ref[...] = jnp.where(z_low, nv_ref[depth - 1], nv_ref[0])

    def pack_body(k, carry):
        b = sblk_ref[k]
        t = ids_ref[k]
        snd_ref[pl.ds(k, 1), :] = jnp.concatenate(
            [nv_ref[b // rows_x, pl.ds(b % rows_x, 1), :], ntv_ref[pl.ds(t, 1), :]], axis=1)
        return carry

    lax.fori_loop(0, slots, pack_body, 0)


def run_step(tables, state, recv, tile_gain, gains_rows, cable_rows, halos):
    volt, recovery, coef_z, coef_x, coef_y, term_volt, term_recovery = state
    depth, rows_x, width = volt.shape
    slots = tables[2].shape[0]
    f32 = jnp.float32
    smem = pl.BlockSpec(memory_space=pltpu.SMEM)
    vmem = pl.BlockSpec(memory_space=pltpu.VMEM)
    out_shape = (
        jax.ShapeDtypeStruct(volt.shape, f32),
        jax.ShapeDtypeStruct(volt.shape, f32),
        jax.ShapeDtypeStruct(term_volt.shape, f32),
        jax.ShapeDtypeStruct(term_volt.shape, f32),
        jax.ShapeDtypeStruct((slots, 2 * width), f32),
        jax.ShapeDtypeStruct((rows_x, width), f32),
        jax.ShapeDtypeStruct((depth, width), f32),
        jax.ShapeDtypeStruct((depth, width), f32),
        jax.ShapeDtypeStruct((depth * rows_x // width, width), f32),
        jax.ShapeDtypeStruct((depth * rows_x // width, width), f32),
    )
    operands = tuple(tables) + (volt, recovery, coef_z, coef_x, coef_y, recv, tile_gain,
                                gains_rows, term_volt, term_recovery, cable_rows) + tuple(halos)
    return pl.pallas_call(
        step_kernel,
        out_shape=out_shape,
        in_specs=[smem] * len(tables) + [vmem] * (len(operands) - len(tables)),
        out_specs=[vmem] * len(out_shape),
        scratch_shapes=[pltpu.VMEM(volt.shape, f32), pltpu.VMEM(term_volt.shape, f32)],
        interpret=INTERPRET,
    )(*operands)


def exchange_halos(faces):
    z_send, x_first, x_last, y_first, y_last = faces
    assert lax.axis_size("gz") == 2
    halos = [lax.ppermute(z_send, "gz", [(0, 1), (1, 0)])]
    for axis, first, last in (("gx", x_first, x_last), ("gy", y_first, y_last)):
        count = lax.axis_size(axis)
        halos.append(lax.ppermute(last, axis, [(i, i + 1) for i in range(count - 1)]))
        halos.append(lax.ppermute(first, axis, [(i + 1, i) for i in range(count - 1)]))
    return halos


def on_device(
    volt,
    recovery,
    fiber_class,
    fiber_table,
    junction_block,
    junction_term,
    junction_owner,
    term_volt,
    term_recovery,
    term_gain,
    cable_gain,
):
    depth, rows_x, width = volt.shape
    owners = lax.axis_size("gx") * lax.axis_size("gy")
    jcount = junction_block.shape[0]
    capacity = max(2, 2 * jcount // owners)
    slots_total = owners * capacity
    term_count = term_volt.shape[0]
    coef_z = jnp.zeros(volt.shape, jnp.float32)
    coef_x = jnp.zeros(volt.shape, jnp.float32)
    coef_y = jnp.zeros(volt.shape, jnp.float32)
    for klass in range(NCLASS):
        hit = fiber_class == klass
        coef_z = jnp.where(hit, fiber_table[0, klass], coef_z)
        coef_x = jnp.where(hit, fiber_table[1, klass], coef_x)
        coef_y = jnp.where(hit, fiber_table[2, klass], coef_y)

    owner = junction_owner[:, 0]
    order = jnp.arange(jcount, dtype=jnp.int32)
    earlier = (owner[:, None] == owner[None, :]) & (order[None, :] < order[:, None])
    rank = jnp.sum(earlier.astype(jnp.int32), axis=1)
    slot = owner * capacity + rank
    hits = slot[None, :] == jnp.arange(slots_total, dtype=jnp.int32)[:, None]
    slot_block = jnp.sum(jnp.where(hits, junction_block[None, :], 0), axis=1)
    slot_term = jnp.sum(jnp.where(hits, junction_term[None, :] + 1, 0), axis=1) - 1

    arrived = lax.all_to_all(slot_term, ("gx", "gy"), split_axis=0, concat_axis=0, tiled=True)
    valid = arrived >= 0
    safe_ids = jnp.where(valid, arrived, 0)
    pick = safe_ids[:, None] == jnp.arange(term_count, dtype=jnp.int32)[None, :]
    gains = jnp.where(valid, jnp.sum(jnp.where(pick, term_gain[None, :], 0.0), axis=1), 0.0)
    gain_rows = jnp.broadcast_to(gains[:, None], (slots_total, width))
    cable_rows = jnp.broadcast_to(cable_gain[:, None], term_volt.shape)

    edges = []
    for axis in ("gz", "gx", "gy"):
        index = lax.axis_index(axis)
        edges += [index == 0, index == lax.axis_size(axis) - 1]
    edges = jnp.stack(edges + edges[:2]).astype(jnp.int32)
    tables = (junction_block, slot, safe_ids, slot_block, edges)

    flat_rows = volt.reshape(depth * rows_x, width)
    sent = jnp.concatenate([flat_rows[slot_block], term_volt[safe_ids], gain_rows], axis=1)
    faces = (
        jnp.where(lax.axis_index("gz") == 0, volt[depth - 1], volt[0]),
        volt[:, 0, :],
        volt[:, rows_x - 1, :],
        volt[:, :, 0].reshape(-1, width),
        volt[:, :, width - 1].reshape(-1, width),
    )
    tile_gain = None
    for step in range(STEPS):
        halos = exchange_halos(faces)
        received = lax.all_to_all(sent, ("gx", "gy"), split_axis=0, concat_axis=0, tiled=True)
        if step == 0:
            tile_gain = received[slot, 2 * width:3 * width]
        state = (volt, recovery, coef_z, coef_x, coef_y, term_volt, term_recovery)
        outs = run_step(tables, state, received, tile_gain, gain_rows, cable_rows, halos)
        volt, recovery, term_volt, term_recovery, sent = outs[:5]
        faces = outs[5:]
    return (volt, recovery, term_volt, term_recovery)


def solution(mesh):
    return jax.shard_map(
        on_device,
        mesh=mesh,
        in_specs=(
            P("gz", "gx", "gy"),
            P("gz", "gx", "gy"),
            P("gz", "gx", "gy"),
            P(),
            P(("gx", "gy", "gz")),
            P(("gx", "gy", "gz")),
            P(("gx", "gy", "gz"), None),
            P(("gx", "gy", "gz"), None),
            P(("gx", "gy", "gz"), None),
            P(("gx", "gy", "gz")),
            P(("gx", "gy", "gz")),
        ),
        out_specs=(
            P("gz", "gx", "gy"),
            P("gz", "gx", "gy"),
            P(("gx", "gy", "gz"), None),
            P(("gx", "gy", "gz"), None),
        ),
        check_vma=False,
    )
```

```python
import jax
import jax.numpy as jnp
from jax import lax
from jax.experimental import pallas as pl
from jax.experimental.pallas import tpu as pltpu
from jax.sharding import PartitionSpec as P

NCLASS = 8
STEPS = 4
INTERPRET = False


def cell_kinetics(v, w, drive):
    react = -8.0 * v * (v - 0.15) * (v - 1.0) - v * w
    new_v = 0.1 * (react + drive)
    new_w = w + 0.01 * (-w - 8.0 * v * (v - 1.15))
    return (new_v, new_w)


def shifted(cells, axis):
    size = cells.shape[axis]
    a = pltpu.roll(cells, 1, axis)
    b = pltpu.roll(cells, size - 1, axis)
    pos = lax.broadcasted_iota(jnp.int32, cells.shape, axis)
    moved = pltpu.roll(pos, 1, axis)
    forward = moved == jnp.where(pos == 0, size - 1, pos - 1)
    return jnp.where(forward, a, b), jnp.where(forward, b, a)


def flag(ref, i, shape):
    return jnp.full(shape, ref[i], jnp.int32) > 0


def step_kernel(
    blk_ref, slot_ref, ids_ref, sblk_ref, edge_ref,
    v_ref, w_ref, cz_ref, cx_ref, cy_ref, recv_ref, tg_ref, g_ref,
    tv_ref, tr_ref, cg_ref, zr_ref, xlo_ref, xhi_ref, ylo_ref, yhi_ref,
    nv_ref, nw_ref, ntv_ref, ntr_ref, snd_ref, zs_ref, xf_ref, xl_ref, yf_ref, yl_ref,
    iv_ref, it_ref,
):
    depth, rows_x, width = v_ref.shape
    jcount = blk_ref.shape[0]
    slots = ids_ref.shape[0]
    iv_ref[...] = jnp.zeros(iv_ref.shape, jnp.float32)
    it_ref[...] = jnp.zeros(it_ref.shape, jnp.float32)

    def tile_body(j, carry):
        b = blk_ref[j]
        s = slot_ref[j]
        z = b // rows_x
        x = b % rows_x
        row = v_ref[z, pl.ds(x, 1), :]
        far = recv_ref[pl.ds(s, 1), :][:, width:2 * width]
        cur = tg_ref[pl.ds(j, 1), :] * (far - row)
        iv_ref[z, pl.ds(x, 1), :] = iv_ref[z, pl.ds(x, 1), :] + cur
        return carry

    lax.fori_loop(0, jcount, tile_body, 0, unroll=8)

    def owner_body(k, carry):
        t = ids_ref[k]
        cur = g_ref[pl.ds(k, 1), :] * (tv_ref[pl.ds(t, 1), :] - recv_ref[pl.ds(k, 1), :][:, 0:width])
        it_ref[pl.ds(t, 1), :] = it_ref[pl.ds(t, 1), :] + (-cur)
        return carry

    lax.fori_loop(0, slots, owner_body, 0, unroll=8)

    u = tv_ref[...]
    r = tr_ref[...]
    u_minus, u_plus = shifted(u, 1)
    lane_t = lax.broadcasted_iota(jnp.int32, u.shape, 1)
    u_minus = jnp.where(lane_t == 0, u, u_minus)
    u_plus = jnp.where(lane_t == width - 1, u, u_plus)
    lap_k = u_plus + u_minus - 2.0 * u
    react_u, new_r = cell_kinetics(u, r, 0.1 * it_ref[...])
    ntv_ref[...] = u + cg_ref[...] * lap_k + react_u
    ntr_ref[...] = new_r

    plane = (rows_x, width)
    sub = lax.broadcasted_iota(jnp.int32, plane, 0)
    lane = lax.broadcasted_iota(jnp.int32, plane, 1)
    z_low = flag(edge_ref, 0, plane)
    z_high = flag(edge_ref, 1, plane)
    x_low = flag(edge_ref, 2, (1, width))
    x_high = flag(edge_ref, 3, (1, width))
    y_low = flag(edge_ref, 4, (rows_x, 1))
    y_high = flag(edge_ref, 5, (rows_x, 1))
    per_row = width // rows_x
    y_first = [jnp.zeros((1, width), jnp.float32) for _ in range(yf_ref.shape[0])]
    y_last = [jnp.zeros((1, width), jnp.float32) for _ in range(yf_ref.shape[0])]
    for z in range(depth):
        vz = v_ref[z]
        if z == 0:
            zm = jnp.where(z_low, vz, zr_ref[...])
        else:
            zm = v_ref[z - 1]
        if z == depth - 1:
            zp = jnp.where(z_high, vz, zr_ref[...])
        else:
            zp = v_ref[z + 1]
        xm, xp = shifted(vz, 0)
        x_lo_row = jnp.where(x_low, vz[0:1, :], xlo_ref[z:z + 1, :])
        x_hi_row = jnp.where(x_high, vz[rows_x - 1:rows_x, :], xhi_ref[z:z + 1, :])
        xm = jnp.where(sub == 0, x_lo_row, xm)
        xp = jnp.where(sub == rows_x - 1, x_hi_row, xp)
        ym, yp = shifted(vz, 1)
        row_at, lane_at = z // per_row, (z % per_row) * rows_x
        pick = lane == sub + lane_at
        y_lo_col = jnp.sum(jnp.where(pick, ylo_ref[row_at:row_at + 1, :], 0.0), axis=1, keepdims=True)
        y_hi_col = jnp.sum(jnp.where(pick, yhi_ref[row_at:row_at + 1, :], 0.0), axis=1, keepdims=True)
        y_lo_col = jnp.where(y_low, vz[:, 0:1], y_lo_col)
        y_hi_col = jnp.where(y_high, vz[:, width - 1:width], y_hi_col)
        ym = jnp.where(lane == 0, y_lo_col, ym)
        yp = jnp.where(lane == width - 1, y_hi_col, yp)
        lap_z = zp + zm - 2.0 * vz
        lap_x = xp + xm - 2.0 * vz
        lap_y = yp + ym - 2.0 * vz
        react_v, new_w = cell_kinetics(vz, w_ref[z], iv_ref[z])
        nv = vz + (cz_ref[z] * lap_z + cx_ref[z] * lap_x + cy_ref[z] * lap_y) + react_v
        nv_ref[z] = nv
        nw_ref[z] = new_w
        xf_ref[z:z + 1, :] = nv[0:1, :]
        xl_ref[z:z + 1, :] = nv[rows_x - 1:rows_x, :]
        y_first[row_at] = y_first[row_at] + jnp.sum(
            jnp.where(pick, nv[:, 0:1], 0.0), axis=0, keepdims=True)
        y_last[row_at] = y_last[row_at] + jnp.sum(
            jnp.where(pick, nv[:, width - 1:width], 0.0), axis=0, keepdims=True)
    for i in range(yf_ref.shape[0]):
        yf_ref[i:i + 1, :] = y_first[i]
        yl_ref[i:i + 1, :] = y_last[i]
    zs_ref[...] = jnp.where(z_low, nv_ref[depth - 1], nv_ref[0])

    def pack_body(k, carry):
        b = sblk_ref[k]
        t = ids_ref[k]
        snd_ref[pl.ds(k, 1), :] = jnp.concatenate(
            [nv_ref[b // rows_x, pl.ds(b % rows_x, 1), :], ntv_ref[pl.ds(t, 1), :]], axis=1)
        return carry

    lax.fori_loop(0, slots, pack_body, 0, unroll=8)


def run_step(tables, state, recv, tile_gain, gains_rows, cable_rows, halos):
    volt, recovery, coef_z, coef_x, coef_y, term_volt, term_recovery = state
    depth, rows_x, width = volt.shape
    slots = tables[2].shape[0]
    f32 = jnp.float32
    smem = pl.BlockSpec(memory_space=pltpu.SMEM)
    vmem = pl.BlockSpec(memory_space=pltpu.VMEM)
    out_shape = (
        jax.ShapeDtypeStruct(volt.shape, f32),
        jax.ShapeDtypeStruct(volt.shape, f32),
        jax.ShapeDtypeStruct(term_volt.shape, f32),
        jax.ShapeDtypeStruct(term_volt.shape, f32),
        jax.ShapeDtypeStruct((slots, 2 * width), f32),
        jax.ShapeDtypeStruct((rows_x, width), f32),
        jax.ShapeDtypeStruct((depth, width), f32),
        jax.ShapeDtypeStruct((depth, width), f32),
        jax.ShapeDtypeStruct((depth * rows_x // width, width), f32),
        jax.ShapeDtypeStruct((depth * rows_x // width, width), f32),
    )
    operands = tuple(tables) + (volt, recovery, coef_z, coef_x, coef_y, recv, tile_gain,
                                gains_rows, term_volt, term_recovery, cable_rows) + tuple(halos)
    return pl.pallas_call(
        step_kernel,
        out_shape=out_shape,
        in_specs=[smem] * len(tables) + [vmem] * (len(operands) - len(tables)),
        out_specs=[vmem] * len(out_shape),
        scratch_shapes=[pltpu.VMEM(volt.shape, f32), pltpu.VMEM(term_volt.shape, f32)],
        interpret=INTERPRET,
    )(*operands)


def exchange_halos(faces):
    z_send, x_first, x_last, y_first, y_last = faces
    assert lax.axis_size("gz") == 2
    halos = [lax.ppermute(z_send, "gz", [(0, 1), (1, 0)])]
    for axis, first, last in (("gx", x_first, x_last), ("gy", y_first, y_last)):
        count = lax.axis_size(axis)
        halos.append(lax.ppermute(last, axis, [(i, i + 1) for i in range(count - 1)]))
        halos.append(lax.ppermute(first, axis, [(i + 1, i) for i in range(count - 1)]))
    return halos


def on_device(
    volt,
    recovery,
    fiber_class,
    fiber_table,
    junction_block,
    junction_term,
    junction_owner,
    term_volt,
    term_recovery,
    term_gain,
    cable_gain,
):
    depth, rows_x, width = volt.shape
    owners = lax.axis_size("gx") * lax.axis_size("gy")
    jcount = junction_block.shape[0]
    capacity = max(2, 2 * jcount // owners)
    slots_total = owners * capacity
    term_count = term_volt.shape[0]
    coef_z = jnp.zeros(volt.shape, jnp.float32)
    coef_x = jnp.zeros(volt.shape, jnp.float32)
    coef_y = jnp.zeros(volt.shape, jnp.float32)
    for klass in range(NCLASS):
        hit = fiber_class == klass
        coef_z = jnp.where(hit, fiber_table[0, klass], coef_z)
        coef_x = jnp.where(hit, fiber_table[1, klass], coef_x)
        coef_y = jnp.where(hit, fiber_table[2, klass], coef_y)

    owner = junction_owner[:, 0]
    order = jnp.arange(jcount, dtype=jnp.int32)
    earlier = (owner[:, None] == owner[None, :]) & (order[None, :] < order[:, None])
    rank = jnp.sum(earlier.astype(jnp.int32), axis=1)
    slot = owner * capacity + rank
    hits = slot[None, :] == jnp.arange(slots_total, dtype=jnp.int32)[:, None]
    slot_block = jnp.sum(jnp.where(hits, junction_block[None, :], 0), axis=1)
    slot_term = jnp.sum(jnp.where(hits, junction_term[None, :] + 1, 0), axis=1) - 1

    arrived = lax.all_to_all(slot_term, ("gx", "gy"), split_axis=0, concat_axis=0, tiled=True)
    valid = arrived >= 0
    safe_ids = jnp.where(valid, arrived, 0)
    pick = safe_ids[:, None] == jnp.arange(term_count, dtype=jnp.int32)[None, :]
    gains = jnp.where(valid, jnp.sum(jnp.where(pick, term_gain[None, :], 0.0), axis=1), 0.0)
    gain_rows = jnp.broadcast_to(gains[:, None], (slots_total, width))
    cable_rows = jnp.broadcast_to(cable_gain[:, None], term_volt.shape)

    edges = []
    for axis in ("gz", "gx", "gy"):
        index = lax.axis_index(axis)
        edges += [index == 0, index == lax.axis_size(axis) - 1]
    edges = jnp.stack(edges + edges[:2]).astype(jnp.int32)
    tables = (junction_block, slot, safe_ids, slot_block, edges)

    flat_rows = volt.reshape(depth * rows_x, width)
    sent = jnp.concatenate([flat_rows[slot_block], term_volt[safe_ids], gain_rows], axis=1)
    faces = (
        jnp.where(lax.axis_index("gz") == 0, volt[depth - 1], volt[0]),
        volt[:, 0, :],
        volt[:, rows_x - 1, :],
        volt[:, :, 0].reshape(-1, width),
        volt[:, :, width - 1].reshape(-1, width),
    )
    tile_gain = None
    for step in range(STEPS):
        halos = exchange_halos(faces)
        received = lax.all_to_all(sent, ("gx", "gy"), split_axis=0, concat_axis=0, tiled=True)
        if step == 0:
            tile_gain = received[:, 2 * width:3 * width][slot]
        state = (volt, recovery, coef_z, coef_x, coef_y, term_volt, term_recovery)
        outs = run_step(tables, state, received, tile_gain, gain_rows, cable_rows, halos)
        volt, recovery, term_volt, term_recovery, sent = outs[:5]
        faces = outs[5:]
    return (volt, recovery, term_volt, term_recovery)


def solution(mesh):
    return jax.shard_map(
        on_device,
        mesh=mesh,
        in_specs=(
            P("gz", "gx", "gy"),
            P("gz", "gx", "gy"),
            P("gz", "gx", "gy"),
            P(),
            P(("gx", "gy", "gz")),
            P(("gx", "gy", "gz")),
            P(("gx", "gy", "gz"), None),
            P(("gx", "gy", "gz"), None),
            P(("gx", "gy", "gz"), None),
            P(("gx", "gy", "gz")),
            P(("gx", "gy", "gz")),
        ),
        out_specs=(
            P("gz", "gx", "gy"),
            P("gz", "gx", "gy"),
            P(("gx", "gy", "gz"), None),
            P(("gx", "gy", "gz"), None),
        ),
        check_vma=False,
    )
```

```python
import jax
import jax.numpy as jnp
from jax import lax
from jax.experimental import pallas as pl
from jax.experimental.pallas import tpu as pltpu
from jax.sharding import PartitionSpec as P

NCLASS = 8
STEPS = 4
INTERPRET = False


def cell_kinetics(v, w, drive):
    react = -8.0 * v * (v - 0.15) * (v - 1.0) - v * w
    new_v = 0.1 * (react + drive)
    new_w = w + 0.01 * (-w - 8.0 * v * (v - 1.15))
    return (new_v, new_w)


def shifted(cells, axis):
    size = cells.shape[axis]
    a = pltpu.roll(cells, 1, axis)
    b = pltpu.roll(cells, size - 1, axis)
    pos = lax.broadcasted_iota(jnp.int32, cells.shape, axis)
    moved = pltpu.roll(pos, 1, axis)
    forward = moved == jnp.where(pos == 0, size - 1, pos - 1)
    return jnp.where(forward, a, b), jnp.where(forward, b, a)


def flag(ref, i, shape):
    return jnp.full(shape, ref[i], jnp.int32) > 0


def split3(x):
    a = x.astype(jnp.bfloat16)
    rest = x - a.astype(jnp.float32)
    b = rest.astype(jnp.bfloat16)
    c = (rest - b.astype(jnp.float32)).astype(jnp.bfloat16)
    return a, b, c


def one_hot_dot(one_hot, x):
    a, b, c = split3(x)
    if INTERPRET:
        one_hot, a, b, c = (t.astype(jnp.float32) for t in (one_hot, a, b, c))
    dot = lambda part: jnp.dot(one_hot, part, preferred_element_type=jnp.float32)
    return (dot(a) + dot(b)) + dot(c)


def step_kernel(
    edge_ref,
    v_ref, w_ref, cz_ref, cx_ref, cy_ref, recv_ref, tg_ref, g_ref,
    tv_ref, tr_ref, cg_ref, zr_ref, xlo_ref, xhi_ref, ylo_ref, yhi_ref,
    oh_blk_ref, oh_blk_t_ref, oh_slot_ref, oh_ids_ref, oh_ids_t_ref, oh_sblk_ref,
    nv_ref, nw_ref, ntv_ref, ntr_ref, snd_ref, zs_ref, xf_ref, xl_ref, yf_ref, yl_ref,
):
    depth, rows_x, width = v_ref.shape

    v_flat = v_ref[...].reshape(depth * rows_x, width)
    rows = one_hot_dot(oh_blk_ref[...], v_flat)
    far = one_hot_dot(oh_slot_ref[...], recv_ref[:, width:2 * width])
    tile_current = tg_ref[...] * (far - rows)
    into_voxel = one_hot_dot(oh_blk_t_ref[...], tile_current)

    far_volt = one_hot_dot(oh_ids_t_ref[...], tv_ref[...])
    current = g_ref[...] * (far_volt - recv_ref[:, 0:width])
    into_term = one_hot_dot(oh_ids_ref[...], -current)

    u = tv_ref[...]
    r = tr_ref[...]
    u_minus, u_plus = shifted(u, 1)
    lane_t = lax.broadcasted_iota(jnp.int32, u.shape, 1)
    u_minus = jnp.where(lane_t == 0, u, u_minus)
    u_plus = jnp.where(lane_t == width - 1, u, u_plus)
    lap_k = u_plus + u_minus - 2.0 * u
    react_u, new_r = cell_kinetics(u, r, 0.1 * into_term)
    ntv_ref[...] = u + cg_ref[...] * lap_k + react_u
    ntr_ref[...] = new_r

    plane = (rows_x, width)
    sub = lax.broadcasted_iota(jnp.int32, plane, 0)
    lane = lax.broadcasted_iota(jnp.int32, plane, 1)
    z_low = flag(edge_ref, 0, plane)
    z_high = flag(edge_ref, 1, plane)
    x_low = flag(edge_ref, 2, (1, width))
    x_high = flag(edge_ref, 3, (1, width))
    y_low = flag(edge_ref, 4, (rows_x, 1))
    y_high = flag(edge_ref, 5, (rows_x, 1))
    per_row = width // rows_x
    y_first = [jnp.zeros((1, width), jnp.float32) for _ in range(yf_ref.shape[0])]
    y_last = [jnp.zeros((1, width), jnp.float32) for _ in range(yf_ref.shape[0])]
    for z in range(depth):
        vz = v_ref[z]
        if z == 0:
            zm = jnp.where(z_low, vz, zr_ref[...])
        else:
            zm = v_ref[z - 1]
        if z == depth - 1:
            zp = jnp.where(z_high, vz, zr_ref[...])
        else:
            zp = v_ref[z + 1]
        xm, xp = shifted(vz, 0)
        x_lo_row = jnp.where(x_low, vz[0:1, :], xlo_ref[z:z + 1, :])
        x_hi_row = jnp.where(x_high, vz[rows_x - 1:rows_x, :], xhi_ref[z:z + 1, :])
        xm = jnp.where(sub == 0, x_lo_row, xm)
        xp = jnp.where(sub == rows_x - 1, x_hi_row, xp)
        ym, yp = shifted(vz, 1)
        row_at, lane_at = z // per_row, (z % per_row) * rows_x
        pick = lane == sub + lane_at
        y_lo_col = jnp.sum(jnp.where(pick, ylo_ref[row_at:row_at + 1, :], 0.0), axis=1, keepdims=True)
        y_hi_col = jnp.sum(jnp.where(pick, yhi_ref[row_at:row_at + 1, :], 0.0), axis=1, keepdims=True)
        y_lo_col = jnp.where(y_low, vz[:, 0:1], y_lo_col)
        y_hi_col = jnp.where(y_high, vz[:, width - 1:width], y_hi_col)
        ym = jnp.where(lane == 0, y_lo_col, ym)
        yp = jnp.where(lane == width - 1, y_hi_col, yp)
        lap_z = zp + zm - 2.0 * vz
        lap_x = xp + xm - 2.0 * vz
        lap_y = yp + ym - 2.0 * vz
        react_v, new_w = cell_kinetics(vz, w_ref[z], into_voxel[z * rows_x:(z + 1) * rows_x])
        nv = vz + (cz_ref[z] * lap_z + cx_ref[z] * lap_x + cy_ref[z] * lap_y) + react_v
        nv_ref[z] = nv
        nw_ref[z] = new_w
        xf_ref[z:z + 1, :] = nv[0:1, :]
        xl_ref[z:z + 1, :] = nv[rows_x - 1:rows_x, :]
        y_first[row_at] = y_first[row_at] + jnp.sum(
            jnp.where(pick, nv[:, 0:1], 0.0), axis=0, keepdims=True)
        y_last[row_at] = y_last[row_at] + jnp.sum(
            jnp.where(pick, nv[:, width - 1:width], 0.0), axis=0, keepdims=True)
    for i in range(yf_ref.shape[0]):
        yf_ref[i:i + 1, :] = y_first[i]
        yl_ref[i:i + 1, :] = y_last[i]
    zs_ref[...] = jnp.where(z_low, nv_ref[depth - 1], nv_ref[0])

    snd_ref[:, 0:width] = one_hot_dot(oh_sblk_ref[...], nv_ref[...].reshape(depth * rows_x, width))
    snd_ref[:, width:2 * width] = one_hot_dot(oh_ids_t_ref[...], ntv_ref[...])


def run_step(tables, state, recv, tile_gain, gains_rows, cable_rows, halos):
    volt, recovery, coef_z, coef_x, coef_y, term_volt, term_recovery = state
    depth, rows_x, width = volt.shape
    slots = recv.shape[0]
    f32 = jnp.float32
    smem = pl.BlockSpec(memory_space=pltpu.SMEM)
    vmem = pl.BlockSpec(memory_space=pltpu.VMEM)
    out_shape = (
        jax.ShapeDtypeStruct(volt.shape, f32),
        jax.ShapeDtypeStruct(volt.shape, f32),
        jax.ShapeDtypeStruct(term_volt.shape, f32),
        jax.ShapeDtypeStruct(term_volt.shape, f32),
        jax.ShapeDtypeStruct((slots, 2 * width), f32),
        jax.ShapeDtypeStruct((rows_x, width), f32),
        jax.ShapeDtypeStruct((depth, width), f32),
        jax.ShapeDtypeStruct((depth, width), f32),
        jax.ShapeDtypeStruct((depth * rows_x // width, width), f32),
        jax.ShapeDtypeStruct((depth * rows_x // width, width), f32),
    )
    edges, one_hots = tables
    operands = (edges, volt, recovery, coef_z, coef_x, coef_y, recv, tile_gain,
                gains_rows, term_volt, term_recovery, cable_rows) + tuple(halos) + tuple(one_hots)
    return pl.pallas_call(
        step_kernel,
        out_shape=out_shape,
        in_specs=[smem] + [vmem] * (len(operands) - 1),
        out_specs=[vmem] * len(out_shape),
        interpret=INTERPRET,
    )(*operands)


def exchange_halos(faces):
    z_send, x_first, x_last, y_first, y_last = faces
    assert lax.axis_size("gz") == 2
    halos = [lax.ppermute(z_send, "gz", [(0, 1), (1, 0)])]
    for axis, first, last in (("gx", x_first, x_last), ("gy", y_first, y_last)):
        count = lax.axis_size(axis)
        halos.append(lax.ppermute(last, axis, [(i, i + 1) for i in range(count - 1)]))
        halos.append(lax.ppermute(first, axis, [(i + 1, i) for i in range(count - 1)]))
    return halos


def on_device(
    volt,
    recovery,
    fiber_class,
    fiber_table,
    junction_block,
    junction_term,
    junction_owner,
    term_volt,
    term_recovery,
    term_gain,
    cable_gain,
):
    depth, rows_x, width = volt.shape
    owners = lax.axis_size("gx") * lax.axis_size("gy")
    jcount = junction_block.shape[0]
    capacity = max(2, 2 * jcount // owners)
    slots_total = owners * capacity
    term_count = term_volt.shape[0]
    coef_z = jnp.zeros(volt.shape, jnp.float32)
    coef_x = jnp.zeros(volt.shape, jnp.float32)
    coef_y = jnp.zeros(volt.shape, jnp.float32)
    for klass in range(NCLASS):
        hit = fiber_class == klass
        coef_z = jnp.where(hit, fiber_table[0, klass], coef_z)
        coef_x = jnp.where(hit, fiber_table[1, klass], coef_x)
        coef_y = jnp.where(hit, fiber_table[2, klass], coef_y)

    owner = junction_owner[:, 0]
    order = jnp.arange(jcount, dtype=jnp.int32)
    earlier = (owner[:, None] == owner[None, :]) & (order[None, :] < order[:, None])
    rank = jnp.sum(earlier.astype(jnp.int32), axis=1)
    slot = owner * capacity + rank
    hits = slot[None, :] == jnp.arange(slots_total, dtype=jnp.int32)[:, None]
    slot_block = jnp.sum(jnp.where(hits, junction_block[None, :], 0), axis=1)
    slot_term = jnp.sum(jnp.where(hits, junction_term[None, :] + 1, 0), axis=1) - 1

    arrived = lax.all_to_all(slot_term, ("gx", "gy"), split_axis=0, concat_axis=0, tiled=True)
    valid = arrived >= 0
    safe_ids = jnp.where(valid, arrived, 0)
    pick = safe_ids[:, None] == jnp.arange(term_count, dtype=jnp.int32)[None, :]
    gains = jnp.where(valid, jnp.sum(jnp.where(pick, term_gain[None, :], 0.0), axis=1), 0.0)
    gain_rows = jnp.broadcast_to(gains[:, None], (slots_total, width))
    cable_rows = jnp.broadcast_to(cable_gain[:, None], term_volt.shape)

    edges = []
    for axis in ("gz", "gx", "gy"):
        index = lax.axis_index(axis)
        edges += [index == 0, index == lax.axis_size(axis) - 1]
    edges = jnp.stack(edges + edges[:2]).astype(jnp.int32)
    bf16 = jnp.bfloat16
    rows_all = jnp.arange(depth * rows_x, dtype=jnp.int32)
    oh_blk = (junction_block[:, None] == rows_all[None, :]).astype(bf16)
    oh_slot = (slot[:, None] == jnp.arange(slots_total, dtype=jnp.int32)[None, :]).astype(bf16)
    oh_ids = (jnp.arange(term_count, dtype=jnp.int32)[:, None] == safe_ids[None, :]).astype(bf16)
    oh_sblk = (slot_block[:, None] == rows_all[None, :]).astype(bf16)
    one_hots = (oh_blk, oh_blk.T, oh_slot, oh_ids, oh_ids.T, oh_sblk)
    tables = (edges, one_hots)

    flat_rows = volt.reshape(depth * rows_x, width)
    sent = jnp.concatenate([flat_rows[slot_block], term_volt[safe_ids], gain_rows], axis=1)
    faces = (
        jnp.where(lax.axis_index("gz") == 0, volt[depth - 1], volt[0]),
        volt[:, 0, :],
        volt[:, rows_x - 1, :],
        volt[:, :, 0].reshape(-1, width),
        volt[:, :, width - 1].reshape(-1, width),
    )
    tile_gain = None
    for step in range(STEPS):
        halos = exchange_halos(faces)
        received = lax.all_to_all(sent, ("gx", "gy"), split_axis=0, concat_axis=0, tiled=True)
        if step == 0:
            tile_gain = received[:, 2 * width:3 * width][slot]
        state = (volt, recovery, coef_z, coef_x, coef_y, term_volt, term_recovery)
        outs = run_step(tables, state, received, tile_gain, gain_rows, cable_rows, halos)
        volt, recovery, term_volt, term_recovery, sent = outs[:5]
        faces = outs[5:]
    return (volt, recovery, term_volt, term_recovery)


def solution(mesh):
    return jax.shard_map(
        on_device,
        mesh=mesh,
        in_specs=(
            P("gz", "gx", "gy"),
            P("gz", "gx", "gy"),
            P("gz", "gx", "gy"),
            P(),
            P(("gx", "gy", "gz")),
            P(("gx", "gy", "gz")),
            P(("gx", "gy", "gz"), None),
            P(("gx", "gy", "gz"), None),
            P(("gx", "gy", "gz"), None),
            P(("gx", "gy", "gz")),
            P(("gx", "gy", "gz")),
        ),
        out_specs=(
            P("gz", "gx", "gy"),
            P("gz", "gx", "gy"),
            P(("gx", "gy", "gz"), None),
            P(("gx", "gy", "gz"), None),
        ),
        check_vma=False,
    )
```

```python
import jax
import jax.numpy as jnp
from jax import lax
from jax.experimental import pallas as pl
from jax.experimental.pallas import tpu as pltpu
from jax.sharding import PartitionSpec as P

NCLASS = 8
STEPS = 4
INTERPRET = False


def cell_kinetics(v, w, drive):
    react = -8.0 * v * (v - 0.15) * (v - 1.0) - v * w
    new_v = 0.1 * (react + drive)
    new_w = w + 0.01 * (-w - 8.0 * v * (v - 1.15))
    return (new_v, new_w)


def shifted(cells, axis):
    size = cells.shape[axis]
    a = pltpu.roll(cells, 1, axis)
    b = pltpu.roll(cells, size - 1, axis)
    pos = lax.broadcasted_iota(jnp.int32, cells.shape, axis)
    moved = pltpu.roll(pos, 1, axis)
    forward = moved == jnp.where(pos == 0, size - 1, pos - 1)
    return jnp.where(forward, a, b), jnp.where(forward, b, a)


def flag(ref, i, shape):
    return jnp.full(shape, ref[i], jnp.int32) > 0


def split3(x):
    a = x.astype(jnp.bfloat16)
    rest = x - a.astype(jnp.float32)
    b = rest.astype(jnp.bfloat16)
    c = (rest - b.astype(jnp.float32)).astype(jnp.bfloat16)
    return a, b, c


def one_hot_dot(one_hot, x):
    a, b, c = split3(x)
    if INTERPRET:
        one_hot, a, b, c = (t.astype(jnp.float32) for t in (one_hot, a, b, c))
    dot = lambda part: jnp.dot(one_hot, part, preferred_element_type=jnp.float32)
    return (dot(a) + dot(b)) + dot(c)


def step_kernel(
    edge_ref,
    v_ref, w_ref, cz_ref, cx_ref, cy_ref, recv_ref, tg_ref, g_ref,
    tv_ref, tr_ref, cg_ref, zr_ref, xlo_ref, xhi_ref, ylo_ref, yhi_ref,
    oh_blk_ref, oh_blk_t_ref, oh_slot_ref, oh_ids_ref, oh_ids_t_ref, oh_sblk_ref,
    nv_ref, nw_ref, ntv_ref, ntr_ref, snd_ref, zs_ref, xf_ref, xl_ref, yf_ref, yl_ref,
):
    depth, rows_x, width = v_ref.shape

    v_flat = v_ref[...].reshape(depth * rows_x, width)
    rows = one_hot_dot(oh_blk_ref[...], v_flat)
    far = one_hot_dot(oh_slot_ref[...], recv_ref[:, width:2 * width])
    tile_current = tg_ref[...] * (far - rows)
    into_voxel = one_hot_dot(oh_blk_t_ref[...], tile_current)

    far_volt = one_hot_dot(oh_ids_t_ref[...], tv_ref[...])
    current = g_ref[...] * (far_volt - recv_ref[:, 0:width])
    into_term = one_hot_dot(oh_ids_ref[...], -current)

    u = tv_ref[...]
    r = tr_ref[...]
    u_minus, u_plus = shifted(u, 1)
    lane_t = lax.broadcasted_iota(jnp.int32, u.shape, 1)
    u_minus = jnp.where(lane_t == 0, u, u_minus)
    u_plus = jnp.where(lane_t == width - 1, u, u_plus)
    lap_k = u_plus + u_minus - 2.0 * u
    react_u, new_r = cell_kinetics(u, r, 0.1 * into_term)
    ntv_ref[...] = u + cg_ref[...] * lap_k + react_u
    ntr_ref[...] = new_r

    plane = (rows_x, width)
    sub = lax.broadcasted_iota(jnp.int32, plane, 0)
    lane = lax.broadcasted_iota(jnp.int32, plane, 1)
    z_low = flag(edge_ref, 0, plane)
    z_high = flag(edge_ref, 1, plane)
    x_low = flag(edge_ref, 2, (1, width))
    x_high = flag(edge_ref, 3, (1, width))
    y_low = flag(edge_ref, 4, (rows_x, 1))
    y_high = flag(edge_ref, 5, (rows_x, 1))
    per_row = width // rows_x
    y_first = [jnp.zeros((1, width), jnp.float32) for _ in range(yf_ref.shape[0])]
    y_last = [jnp.zeros((1, width), jnp.float32) for _ in range(yf_ref.shape[0])]
    for z in range(depth):
        vz = v_ref[z]
        if z == 0:
            zm = jnp.where(z_low, vz, zr_ref[...])
        else:
            zm = v_ref[z - 1]
        if z == depth - 1:
            zp = jnp.where(z_high, vz, zr_ref[...])
        else:
            zp = v_ref[z + 1]
        xm, xp = shifted(vz, 0)
        x_lo_row = jnp.where(x_low, vz[0:1, :], xlo_ref[z:z + 1, :])
        x_hi_row = jnp.where(x_high, vz[rows_x - 1:rows_x, :], xhi_ref[z:z + 1, :])
        xm = jnp.where(sub == 0, x_lo_row, xm)
        xp = jnp.where(sub == rows_x - 1, x_hi_row, xp)
        ym, yp = shifted(vz, 1)
        row_at, lane_at = z // per_row, (z % per_row) * rows_x
        pick = lane == sub + lane_at
        y_lo_col = jnp.sum(jnp.where(pick, ylo_ref[row_at:row_at + 1, :], 0.0), axis=1, keepdims=True)
        y_hi_col = jnp.sum(jnp.where(pick, yhi_ref[row_at:row_at + 1, :], 0.0), axis=1, keepdims=True)
        y_lo_col = jnp.where(y_low, vz[:, 0:1], y_lo_col)
        y_hi_col = jnp.where(y_high, vz[:, width - 1:width], y_hi_col)
        ym = jnp.where(lane == 0, y_lo_col, ym)
        yp = jnp.where(lane == width - 1, y_hi_col, yp)
        lap_z = zp + zm - 2.0 * vz
        lap_x = xp + xm - 2.0 * vz
        lap_y = yp + ym - 2.0 * vz
        react_v, new_w = cell_kinetics(vz, w_ref[z], into_voxel[z * rows_x:(z + 1) * rows_x])
        nv = vz + (cz_ref[z] * lap_z + cx_ref[z] * lap_x + cy_ref[z] * lap_y) + react_v
        nv_ref[z] = nv
        nw_ref[z] = new_w
        xf_ref[z:z + 1, :] = nv[0:1, :]
        xl_ref[z:z + 1, :] = nv[rows_x - 1:rows_x, :]
        y_first[row_at] = y_first[row_at] + jnp.sum(
            jnp.where(pick, nv[:, 0:1], 0.0), axis=0, keepdims=True)
        y_last[row_at] = y_last[row_at] + jnp.sum(
            jnp.where(pick, nv[:, width - 1:width], 0.0), axis=0, keepdims=True)
    for i in range(yf_ref.shape[0]):
        yf_ref[i:i + 1, :] = y_first[i]
        yl_ref[i:i + 1, :] = y_last[i]
    zs_ref[...] = jnp.where(z_low, nv_ref[depth - 1], nv_ref[0])

    snd_ref[:, 0:width] = one_hot_dot(oh_sblk_ref[...], nv_ref[...].reshape(depth * rows_x, width))
    snd_ref[:, width:2 * width] = one_hot_dot(oh_ids_t_ref[...], ntv_ref[...])


def coef_kernel(table_ref, cls_ref, cz_ref, cx_ref, cy_ref):
    for z in range(cls_ref.shape[0]):
        klass = cls_ref[z]
        outs = [jnp.zeros(klass.shape, jnp.float32) for _ in range(3)]
        for k in range(NCLASS):
            hit = klass == k
            outs = [jnp.where(hit, table_ref[d, k], outs[d]) for d in range(3)]
        cz_ref[z], cx_ref[z], cy_ref[z] = outs


def coefficients(fiber_class, fiber_table):
    shape = jax.ShapeDtypeStruct(fiber_class.shape, jnp.float32)
    vmem = pl.BlockSpec(memory_space=pltpu.VMEM)
    return pl.pallas_call(
        coef_kernel,
        out_shape=(shape, shape, shape),
        in_specs=[pl.BlockSpec(memory_space=pltpu.SMEM), vmem],
        out_specs=[vmem] * 3,
        interpret=INTERPRET,
    )(fiber_table, fiber_class)


def run_step(tables, state, recv, tile_gain, gains_rows, cable_rows, halos):
    volt, recovery, coef_z, coef_x, coef_y, term_volt, term_recovery = state
    depth, rows_x, width = volt.shape
    slots = recv.shape[0]
    f32 = jnp.float32
    smem = pl.BlockSpec(memory_space=pltpu.SMEM)
    vmem = pl.BlockSpec(memory_space=pltpu.VMEM)
    out_shape = (
        jax.ShapeDtypeStruct(volt.shape, f32),
        jax.ShapeDtypeStruct(volt.shape, f32),
        jax.ShapeDtypeStruct(term_volt.shape, f32),
        jax.ShapeDtypeStruct(term_volt.shape, f32),
        jax.ShapeDtypeStruct((slots, 2 * width), f32),
        jax.ShapeDtypeStruct((rows_x, width), f32),
        jax.ShapeDtypeStruct((depth, width), f32),
        jax.ShapeDtypeStruct((depth, width), f32),
        jax.ShapeDtypeStruct((depth * rows_x // width, width), f32),
        jax.ShapeDtypeStruct((depth * rows_x // width, width), f32),
    )
    edges, one_hots = tables
    operands = (edges, volt, recovery, coef_z, coef_x, coef_y, recv, tile_gain,
                gains_rows, term_volt, term_recovery, cable_rows) + tuple(halos) + tuple(one_hots)
    return pl.pallas_call(
        step_kernel,
        out_shape=out_shape,
        in_specs=[smem] + [vmem] * (len(operands) - 1),
        out_specs=[vmem] * len(out_shape),
        interpret=INTERPRET,
    )(*operands)


def exchange_halos(faces):
    z_send, x_first, x_last, y_first, y_last = faces
    assert lax.axis_size("gz") == 2
    halos = [lax.ppermute(z_send, "gz", [(0, 1), (1, 0)])]
    for axis, first, last in (("gx", x_first, x_last), ("gy", y_first, y_last)):
        count = lax.axis_size(axis)
        halos.append(lax.ppermute(last, axis, [(i, i + 1) for i in range(count - 1)]))
        halos.append(lax.ppermute(first, axis, [(i + 1, i) for i in range(count - 1)]))
    return halos


def on_device(
    volt,
    recovery,
    fiber_class,
    fiber_table,
    junction_block,
    junction_term,
    junction_owner,
    term_volt,
    term_recovery,
    term_gain,
    cable_gain,
):
    depth, rows_x, width = volt.shape
    owners = lax.axis_size("gx") * lax.axis_size("gy")
    jcount = junction_block.shape[0]
    capacity = max(2, 2 * jcount // owners)
    slots_total = owners * capacity
    term_count = term_volt.shape[0]
    coef_z, coef_x, coef_y = coefficients(fiber_class, fiber_table)

    owner = junction_owner[:, 0]
    order = jnp.arange(jcount, dtype=jnp.int32)
    earlier = (owner[:, None] == owner[None, :]) & (order[None, :] < order[:, None])
    rank = jnp.sum(earlier.astype(jnp.int32), axis=1)
    slot = owner * capacity + rank
    hits = slot[None, :] == jnp.arange(slots_total, dtype=jnp.int32)[:, None]
    slot_block = jnp.sum(jnp.where(hits, junction_block[None, :], 0), axis=1)
    slot_term = jnp.sum(jnp.where(hits, junction_term[None, :] + 1, 0), axis=1) - 1

    arrived = lax.all_to_all(slot_term, ("gx", "gy"), split_axis=0, concat_axis=0, tiled=True)
    valid = arrived >= 0
    safe_ids = jnp.where(valid, arrived, 0)
    pick = safe_ids[:, None] == jnp.arange(term_count, dtype=jnp.int32)[None, :]
    gains = jnp.where(valid, jnp.sum(jnp.where(pick, term_gain[None, :], 0.0), axis=1), 0.0)
    gain_rows = jnp.broadcast_to(gains[:, None], (slots_total, width))
    cable_rows = jnp.broadcast_to(cable_gain[:, None], term_volt.shape)

    edges = []
    for axis in ("gz", "gx", "gy"):
        index = lax.axis_index(axis)
        edges += [index == 0, index == lax.axis_size(axis) - 1]
    edges = jnp.stack(edges + edges[:2]).astype(jnp.int32)
    bf16 = jnp.bfloat16
    rows_all = jnp.arange(depth * rows_x, dtype=jnp.int32)
    oh_blk = (junction_block[:, None] == rows_all[None, :]).astype(bf16)
    oh_slot = (slot[:, None] == jnp.arange(slots_total, dtype=jnp.int32)[None, :]).astype(bf16)
    oh_ids = (jnp.arange(term_count, dtype=jnp.int32)[:, None] == safe_ids[None, :]).astype(bf16)
    oh_sblk = (slot_block[:, None] == rows_all[None, :]).astype(bf16)
    one_hots = (oh_blk, oh_blk.T, oh_slot, oh_ids, oh_ids.T, oh_sblk)
    tables = (edges, one_hots)

    flat_rows = volt.reshape(depth * rows_x, width)
    sent = jnp.concatenate([flat_rows[slot_block], term_volt[safe_ids], gain_rows], axis=1)
    faces = (
        jnp.where(lax.axis_index("gz") == 0, volt[depth - 1], volt[0]),
        volt[:, 0, :],
        volt[:, rows_x - 1, :],
        volt[:, :, 0].reshape(-1, width),
        volt[:, :, width - 1].reshape(-1, width),
    )
    faces, sent = lax.optimization_barrier((faces, sent))
    tile_gain = None
    for step in range(STEPS):
        halos = exchange_halos(faces)
        received = lax.all_to_all(sent, ("gx", "gy"), split_axis=0, concat_axis=0, tiled=True)
        if step == 0:
            tile_gain = received[:, 2 * width:3 * width][slot]
        state = (volt, recovery, coef_z, coef_x, coef_y, term_volt, term_recovery)
        outs = run_step(tables, state, received, tile_gain, gain_rows, cable_rows, halos)
        volt, recovery, term_volt, term_recovery, sent = outs[:5]
        faces = outs[5:]
    return (volt, recovery, term_volt, term_recovery)


def solution(mesh):
    return jax.shard_map(
        on_device,
        mesh=mesh,
        in_specs=(
            P("gz", "gx", "gy"),
            P("gz", "gx", "gy"),
            P("gz", "gx", "gy"),
            P(),
            P(("gx", "gy", "gz")),
            P(("gx", "gy", "gz")),
            P(("gx", "gy", "gz"), None),
            P(("gx", "gy", "gz"), None),
            P(("gx", "gy", "gz"), None),
            P(("gx", "gy", "gz")),
            P(("gx", "gy", "gz")),
        ),
        out_specs=(
            P("gz", "gx", "gy"),
            P("gz", "gx", "gy"),
            P(("gx", "gy", "gz"), None),
            P(("gx", "gy", "gz"), None),
        ),
        check_vma=False,
    )
```

```python
import functools

import jax
import jax.numpy as jnp
from jax import lax
from jax.experimental import pallas as pl
from jax.experimental.pallas import tpu as pltpu
from jax.sharding import PartitionSpec as P

NCLASS = 8
STEPS = 4
INTERPRET = False


def cell_kinetics(v, w, drive):
    react = -8.0 * v * (v - 0.15) * (v - 1.0) - v * w
    new_v = 0.1 * (react + drive)
    new_w = w + 0.01 * (-w - 8.0 * v * (v - 1.15))
    return (new_v, new_w)


def shifted(cells, axis):
    size = cells.shape[axis]
    a = pltpu.roll(cells, 1, axis)
    b = pltpu.roll(cells, size - 1, axis)
    pos = lax.broadcasted_iota(jnp.int32, cells.shape, axis)
    moved = pltpu.roll(pos, 1, axis)
    forward = moved == jnp.where(pos == 0, size - 1, pos - 1)
    return jnp.where(forward, a, b), jnp.where(forward, b, a)


def flag(ref, i, shape):
    return jnp.full(shape, ref[i], jnp.int32) > 0


def split3(x):
    a = x.astype(jnp.bfloat16)
    rest = x - a.astype(jnp.float32)
    b = rest.astype(jnp.bfloat16)
    c = (rest - b.astype(jnp.float32)).astype(jnp.bfloat16)
    return a, b, c


def one_hot_dot(one_hot, x):
    a, b, c = split3(x)
    if INTERPRET:
        one_hot, a, b, c = (t.astype(jnp.float32) for t in (one_hot, a, b, c))
    dot = lambda part: jnp.dot(one_hot, part, preferred_element_type=jnp.float32)
    return (dot(a) + dot(b)) + dot(c)


def slab_kernel(
    edge_ref, v_ref, w_ref, cz_ref, cx_ref, cy_ref, zr_ref, xlo_ref, xhi_ref, ylo_ref, yhi_ref,
    base_ref, react_ref, nw_ref,
):
    depth, rows_x, width = v_ref.shape
    plane = (rows_x, width)
    sub = lax.broadcasted_iota(jnp.int32, plane, 0)
    lane = lax.broadcasted_iota(jnp.int32, plane, 1)
    z_low = flag(edge_ref, 0, plane)
    z_high = flag(edge_ref, 1, plane)
    x_low = flag(edge_ref, 2, (1, width))
    x_high = flag(edge_ref, 3, (1, width))
    y_low = flag(edge_ref, 4, (rows_x, 1))
    y_high = flag(edge_ref, 5, (rows_x, 1))
    per_row = width // rows_x
    for z in range(depth):
        vz = v_ref[z]
        if z == 0:
            zm = jnp.where(z_low, vz, zr_ref[...])
        else:
            zm = v_ref[z - 1]
        if z == depth - 1:
            zp = jnp.where(z_high, vz, zr_ref[...])
        else:
            zp = v_ref[z + 1]
        xm, xp = shifted(vz, 0)
        x_lo_row = jnp.where(x_low, vz[0:1, :], xlo_ref[z:z + 1, :])
        x_hi_row = jnp.where(x_high, vz[rows_x - 1:rows_x, :], xhi_ref[z:z + 1, :])
        xm = jnp.where(sub == 0, x_lo_row, xm)
        xp = jnp.where(sub == rows_x - 1, x_hi_row, xp)
        ym, yp = shifted(vz, 1)
        row_at, lane_at = z // per_row, (z % per_row) * rows_x
        pick = lane == sub + lane_at
        y_lo_col = jnp.sum(jnp.where(pick, ylo_ref[row_at:row_at + 1, :], 0.0), axis=1, keepdims=True)
        y_hi_col = jnp.sum(jnp.where(pick, yhi_ref[row_at:row_at + 1, :], 0.0), axis=1, keepdims=True)
        y_lo_col = jnp.where(y_low, vz[:, 0:1], y_lo_col)
        y_hi_col = jnp.where(y_high, vz[:, width - 1:width], y_hi_col)
        ym = jnp.where(lane == 0, y_lo_col, ym)
        yp = jnp.where(lane == width - 1, y_hi_col, yp)
        lap_z = zp + zm - 2.0 * vz
        lap_x = xp + xm - 2.0 * vz
        lap_y = yp + ym - 2.0 * vz
        wz = w_ref[z]
        base_ref[z] = vz + (cz_ref[z] * lap_z + cx_ref[z] * lap_x + cy_ref[z] * lap_y)
        react_ref[z] = -8.0 * vz * (vz - 0.15) * (vz - 1.0) - vz * wz
        nw_ref[z] = wz + 0.01 * (-wz - 8.0 * vz * (vz - 1.15))


def junction_kernel(
    edge_ref,
    v_ref, base_ref, react_ref, recv_ref, tg_ref, g_ref, tv_ref, tr_ref, cg_ref,
    oh_blk_ref, oh_blk_t_ref, oh_slot_ref, oh_ids_ref, oh_ids_t_ref, oh_sblk_ref,
    nv_ref, ntv_ref, ntr_ref, *tail, pack,
):
    depth, rows_x, width = v_ref.shape

    v_flat = v_ref[...].reshape(depth * rows_x, width)
    rows = one_hot_dot(oh_blk_ref[...], v_flat)
    far = one_hot_dot(oh_slot_ref[...], recv_ref[:, width:2 * width])
    tile_current = tg_ref[...] * (far - rows)
    into_voxel = one_hot_dot(oh_blk_t_ref[...], tile_current).reshape(depth, rows_x, width)
    nv = base_ref[...] + 0.1 * (react_ref[...] + into_voxel)
    nv_ref[...] = nv

    far_volt = one_hot_dot(oh_ids_t_ref[...], tv_ref[...])
    current = g_ref[...] * (far_volt - recv_ref[:, 0:width])
    into_term = one_hot_dot(oh_ids_ref[...], -current)

    u = tv_ref[...]
    r = tr_ref[...]
    u_minus, u_plus = shifted(u, 1)
    lane_t = lax.broadcasted_iota(jnp.int32, u.shape, 1)
    u_minus = jnp.where(lane_t == 0, u, u_minus)
    u_plus = jnp.where(lane_t == width - 1, u, u_plus)
    lap_k = u_plus + u_minus - 2.0 * u
    react_u, new_r = cell_kinetics(u, r, 0.1 * into_term)
    ntv = u + cg_ref[...] * lap_k + react_u
    ntv_ref[...] = ntv
    ntr_ref[...] = new_r
    if not pack:
        return
    snd_ref, zs_ref, xf_ref, xl_ref, yf_ref, yl_ref = tail

    plane = (rows_x, width)
    sub = lax.broadcasted_iota(jnp.int32, plane, 0)
    lane = lax.broadcasted_iota(jnp.int32, plane, 1)
    per_row = width // rows_x
    y_first = [jnp.zeros((1, width), jnp.float32) for _ in range(yf_ref.shape[0])]
    y_last = [jnp.zeros((1, width), jnp.float32) for _ in range(yf_ref.shape[0])]
    for z in range(depth):
        nz = nv[z]
        xf_ref[z:z + 1, :] = nz[0:1, :]
        xl_ref[z:z + 1, :] = nz[rows_x - 1:rows_x, :]
        row_at, lane_at = z // per_row, (z % per_row) * rows_x
        pick = lane == sub + lane_at
        y_first[row_at] = y_first[row_at] + jnp.sum(
            jnp.where(pick, nz[:, 0:1], 0.0), axis=0, keepdims=True)
        y_last[row_at] = y_last[row_at] + jnp.sum(
            jnp.where(pick, nz[:, width - 1:width], 0.0), axis=0, keepdims=True)
    for i in range(yf_ref.shape[0]):
        yf_ref[i:i + 1, :] = y_first[i]
        yl_ref[i:i + 1, :] = y_last[i]
    zs_ref[...] = jnp.where(flag(edge_ref, 0, plane), nv[depth - 1], nv[0])

    snd_ref[:, 0:width] = one_hot_dot(oh_sblk_ref[...], nv.reshape(depth * rows_x, width))
    snd_ref[:, width:2 * width] = one_hot_dot(oh_ids_t_ref[...], ntv)


def coef_kernel(table_ref, cls_ref, cz_ref, cx_ref, cy_ref):
    for z in range(cls_ref.shape[0]):
        klass = cls_ref[z]
        outs = [jnp.zeros(klass.shape, jnp.float32) for _ in range(3)]
        for k in range(NCLASS):
            hit = klass == k
            outs = [jnp.where(hit, table_ref[d, k], outs[d]) for d in range(3)]
        cz_ref[z], cx_ref[z], cy_ref[z] = outs


def coefficients(fiber_class, fiber_table):
    shape = jax.ShapeDtypeStruct(fiber_class.shape, jnp.float32)
    vmem = pl.BlockSpec(memory_space=pltpu.VMEM)
    return pl.pallas_call(
        coef_kernel,
        out_shape=(shape, shape, shape),
        in_specs=[pl.BlockSpec(memory_space=pltpu.SMEM), vmem],
        out_specs=[vmem] * 3,
        interpret=INTERPRET,
    )(fiber_table, fiber_class)


def run_step(tables, state, recv, tile_gain, gains_rows, cable_rows, halos, pack):
    volt, recovery, coef_z, coef_x, coef_y, term_volt, term_recovery = state
    depth, rows_x, width = volt.shape
    slots = recv.shape[0]
    edges, one_hots = tables
    f32 = jnp.float32
    smem = pl.BlockSpec(memory_space=pltpu.SMEM)
    vmem = pl.BlockSpec(memory_space=pltpu.VMEM)
    slab = jax.ShapeDtypeStruct(volt.shape, f32)
    operands = (edges, volt, recovery, coef_z, coef_x, coef_y) + tuple(halos)
    base, react, new_w = pl.pallas_call(
        slab_kernel,
        out_shape=(slab, slab, slab),
        in_specs=[smem] + [vmem] * (len(operands) - 1),
        out_specs=[vmem] * 3,
        interpret=INTERPRET,
    )(*operands)
    term = jax.ShapeDtypeStruct(term_volt.shape, f32)
    out_shape = (slab, term, term)
    if pack:
        out_shape += (
            jax.ShapeDtypeStruct((slots, 2 * width), f32),
            jax.ShapeDtypeStruct((rows_x, width), f32),
            jax.ShapeDtypeStruct((depth, width), f32),
            jax.ShapeDtypeStruct((depth, width), f32),
            jax.ShapeDtypeStruct((depth * rows_x // width, width), f32),
            jax.ShapeDtypeStruct((depth * rows_x // width, width), f32),
        )
    operands = (edges, volt, base, react, recv, tile_gain, gains_rows, term_volt, term_recovery,
                cable_rows) + tuple(one_hots)
    outs = pl.pallas_call(
        functools.partial(junction_kernel, pack=pack),
        out_shape=out_shape,
        in_specs=[smem] + [vmem] * (len(operands) - 1),
        out_specs=[vmem] * len(out_shape),
        interpret=INTERPRET,
    )(*operands)
    return (outs[0], new_w) + tuple(outs[1:])


def exchange_halos(faces):
    z_send, x_first, x_last, y_first, y_last = faces
    assert lax.axis_size("gz") == 2
    halos = [lax.ppermute(z_send, "gz", [(0, 1), (1, 0)])]
    for axis, first, last in (("gx", x_first, x_last), ("gy", y_first, y_last)):
        count = lax.axis_size(axis)
        halos.append(lax.ppermute(last, axis, [(i, i + 1) for i in range(count - 1)]))
        halos.append(lax.ppermute(first, axis, [(i + 1, i) for i in range(count - 1)]))
    return halos


def on_device(
    volt,
    recovery,
    fiber_class,
    fiber_table,
    junction_block,
    junction_term,
    junction_owner,
    term_volt,
    term_recovery,
    term_gain,
    cable_gain,
):
    depth, rows_x, width = volt.shape
    owners = lax.axis_size("gx") * lax.axis_size("gy")
    jcount = junction_block.shape[0]
    capacity = max(2, 2 * jcount // owners)
    slots_total = owners * capacity
    term_count = term_volt.shape[0]
    coef_z, coef_x, coef_y = coefficients(fiber_class, fiber_table)

    owner = junction_owner[:, 0]
    order = jnp.arange(jcount, dtype=jnp.int32)
    earlier = (owner[:, None] == owner[None, :]) & (order[None, :] < order[:, None])
    rank = jnp.sum(earlier.astype(jnp.int32), axis=1)
    slot = owner * capacity + rank
    hits = slot[None, :] == jnp.arange(slots_total, dtype=jnp.int32)[:, None]
    slot_block = jnp.sum(jnp.where(hits, junction_block[None, :], 0), axis=1)
    slot_term = jnp.sum(jnp.where(hits, junction_term[None, :] + 1, 0), axis=1) - 1

    arrived = lax.all_to_all(slot_term, ("gx", "gy"), split_axis=0, concat_axis=0, tiled=True)
    valid = arrived >= 0
    safe_ids = jnp.where(valid, arrived, 0)
    pick = safe_ids[:, None] == jnp.arange(term_count, dtype=jnp.int32)[None, :]
    gains = jnp.where(valid, jnp.sum(jnp.where(pick, term_gain[None, :], 0.0), axis=1), 0.0)
    gain_rows = jnp.broadcast_to(gains[:, None], (slots_total, width))
    cable_rows = jnp.broadcast_to(cable_gain[:, None], term_volt.shape)

    edges = []
    for axis in ("gz", "gx", "gy"):
        index = lax.axis_index(axis)
        edges += [index == 0, index == lax.axis_size(axis) - 1]
    edges = jnp.stack(edges + edges[:2]).astype(jnp.int32)
    bf16 = jnp.bfloat16
    rows_all = jnp.arange(depth * rows_x, dtype=jnp.int32)
    oh_blk = (junction_block[:, None] == rows_all[None, :]).astype(bf16)
    oh_slot = (slot[:, None] == jnp.arange(slots_total, dtype=jnp.int32)[None, :]).astype(bf16)
    oh_ids = (jnp.arange(term_count, dtype=jnp.int32)[:, None] == safe_ids[None, :]).astype(bf16)
    oh_sblk = (slot_block[:, None] == rows_all[None, :]).astype(bf16)
    one_hots = (oh_blk, oh_blk.T, oh_slot, oh_ids, oh_ids.T, oh_sblk)
    tables = (edges, one_hots)

    flat_rows = volt.reshape(depth * rows_x, width)
    sent = jnp.concatenate([flat_rows[slot_block], term_volt[safe_ids], gain_rows], axis=1)
    faces = (
        jnp.where(lax.axis_index("gz") == 0, volt[depth - 1], volt[0]),
        volt[:, 0, :],
        volt[:, rows_x - 1, :],
        volt[:, :, 0].reshape(-1, width),
        volt[:, :, width - 1].reshape(-1, width),
    )
    faces, sent = lax.optimization_barrier((faces, sent))
    tile_gain = None
    for step in range(STEPS):
        halos = exchange_halos(faces)
        received = lax.all_to_all(sent, ("gx", "gy"), split_axis=0, concat_axis=0, tiled=True)
        if step == 0:
            tile_gain = received[:, 2 * width:3 * width][slot]
        state = (volt, recovery, coef_z, coef_x, coef_y, term_volt, term_recovery)
        outs = run_step(tables, state, received, tile_gain, gain_rows, cable_rows, halos, step < STEPS - 1)
        volt, recovery, term_volt, term_recovery = outs[:4]
        sent, faces = (outs[4], outs[5:]) if step < STEPS - 1 else (None, None)
    return (volt, recovery, term_volt, term_recovery)


def solution(mesh):
    return jax.shard_map(
        on_device,
        mesh=mesh,
        in_specs=(
            P("gz", "gx", "gy"),
            P("gz", "gx", "gy"),
            P("gz", "gx", "gy"),
            P(),
            P(("gx", "gy", "gz")),
            P(("gx", "gy", "gz")),
            P(("gx", "gy", "gz"), None),
            P(("gx", "gy", "gz"), None),
            P(("gx", "gy", "gz"), None),
            P(("gx", "gy", "gz")),
            P(("gx", "gy", "gz")),
        ),
        out_specs=(
            P("gz", "gx", "gy"),
            P("gz", "gx", "gy"),
            P(("gx", "gy", "gz"), None),
            P(("gx", "gy", "gz"), None),
        ),
        check_vma=False,
    )
```

```python
import functools

import jax
import jax.numpy as jnp
from jax import lax
from jax.experimental import pallas as pl
from jax.experimental.pallas import tpu as pltpu
from jax.sharding import PartitionSpec as P

NCLASS = 8
STEPS = 4
INTERPRET = False


def cell_kinetics(v, w, drive):
    react = -8.0 * v * (v - 0.15) * (v - 1.0) - v * w
    new_v = 0.1 * (react + drive)
    new_w = w + 0.01 * (-w - 8.0 * v * (v - 1.15))
    return (new_v, new_w)


def shifted(cells, axis):
    size = cells.shape[axis]
    a = pltpu.roll(cells, 1, axis)
    b = pltpu.roll(cells, size - 1, axis)
    pos = lax.broadcasted_iota(jnp.int32, cells.shape, axis)
    moved = pltpu.roll(pos, 1, axis)
    forward = moved == jnp.where(pos == 0, size - 1, pos - 1)
    return jnp.where(forward, a, b), jnp.where(forward, b, a)


def flag(ref, i, shape):
    return jnp.full(shape, ref[i], jnp.int32) > 0


def split3(x):
    a = x.astype(jnp.bfloat16)
    rest = x - a.astype(jnp.float32)
    b = rest.astype(jnp.bfloat16)
    c = (rest - b.astype(jnp.float32)).astype(jnp.bfloat16)
    return a, b, c


def one_hot_dot(one_hot, x):
    a, b, c = split3(x)
    if INTERPRET:
        one_hot, a, b, c = (t.astype(jnp.float32) for t in (one_hot, a, b, c))
    dot = lambda part: jnp.dot(one_hot, part, preferred_element_type=jnp.float32)
    return (dot(a) + dot(b)) + dot(c)


def step_kernel(*refs, first, pack):
    refs = iter(refs)
    edge_ref, v_ref, w_ref, cz_ref, cx_ref, cy_ref, recv_ref = (next(refs) for _ in range(7))
    tg_ref = None if first else next(refs)
    g_ref, tv_ref, tr_ref, cg_ref, zr_ref, xlo_ref, xhi_ref, ylo_ref, yhi_ref = (next(refs) for _ in range(9))
    oh_blk_ref, oh_blk_t_ref, oh_slot_ref, oh_ids_ref, oh_ids_t_ref, oh_sblk_ref = (next(refs) for _ in range(6))
    nv_ref, nw_ref, ntv_ref, ntr_ref = (next(refs) for _ in range(4))
    if pack:
        snd_ref, zs_ref, xf_ref, xl_ref, yf_ref, yl_ref = (next(refs) for _ in range(6))
    depth, rows_x, width = v_ref.shape
    if first:
        tile_gain = one_hot_dot(oh_slot_ref[...], recv_ref[:, 2 * width:3 * width])
        next(refs)[...] = tile_gain
    else:
        tile_gain = tg_ref[...]

    v_flat = v_ref[...].reshape(depth * rows_x, width)
    rows = one_hot_dot(oh_blk_ref[...], v_flat)
    far = one_hot_dot(oh_slot_ref[...], recv_ref[:, width:2 * width])
    tile_current = tile_gain * (far - rows)
    into_voxel = one_hot_dot(oh_blk_t_ref[...], tile_current)

    far_volt = one_hot_dot(oh_ids_t_ref[...], tv_ref[...])
    current = g_ref[...] * (far_volt - recv_ref[:, 0:width])
    into_term = one_hot_dot(oh_ids_ref[...], -current)

    u = tv_ref[...]
    r = tr_ref[...]
    u_minus, u_plus = shifted(u, 1)
    lane_t = lax.broadcasted_iota(jnp.int32, u.shape, 1)
    u_minus = jnp.where(lane_t == 0, u, u_minus)
    u_plus = jnp.where(lane_t == width - 1, u, u_plus)
    lap_k = u_plus + u_minus - 2.0 * u
    react_u, new_r = cell_kinetics(u, r, 0.1 * into_term)
    ntv_ref[...] = u + cg_ref[...] * lap_k + react_u
    ntr_ref[...] = new_r

    plane = (rows_x, width)
    sub = lax.broadcasted_iota(jnp.int32, plane, 0)
    lane = lax.broadcasted_iota(jnp.int32, plane, 1)
    z_low = flag(edge_ref, 0, plane)
    z_high = flag(edge_ref, 1, plane)
    x_low = flag(edge_ref, 2, (1, width))
    x_high = flag(edge_ref, 3, (1, width))
    y_low = flag(edge_ref, 4, (rows_x, 1))
    y_high = flag(edge_ref, 5, (rows_x, 1))
    per_row = width // rows_x
    face_rows = depth * rows_x // width
    y_first = [jnp.zeros((1, width), jnp.float32) for _ in range(face_rows)]
    y_last = [jnp.zeros((1, width), jnp.float32) for _ in range(face_rows)]
    for z in range(depth):
        vz = v_ref[z]
        if z == 0:
            zm = jnp.where(z_low, vz, zr_ref[...])
        else:
            zm = v_ref[z - 1]
        if z == depth - 1:
            zp = jnp.where(z_high, vz, zr_ref[...])
        else:
            zp = v_ref[z + 1]
        xm, xp = shifted(vz, 0)
        x_lo_row = jnp.where(x_low, vz[0:1, :], xlo_ref[z:z + 1, :])
        x_hi_row = jnp.where(x_high, vz[rows_x - 1:rows_x, :], xhi_ref[z:z + 1, :])
        xm = jnp.where(sub == 0, x_lo_row, xm)
        xp = jnp.where(sub == rows_x - 1, x_hi_row, xp)
        ym, yp = shifted(vz, 1)
        row_at, lane_at = z // per_row, (z % per_row) * rows_x
        pick = lane == sub + lane_at
        y_lo_col = jnp.sum(jnp.where(pick, ylo_ref[row_at:row_at + 1, :], 0.0), axis=1, keepdims=True)
        y_hi_col = jnp.sum(jnp.where(pick, yhi_ref[row_at:row_at + 1, :], 0.0), axis=1, keepdims=True)
        y_lo_col = jnp.where(y_low, vz[:, 0:1], y_lo_col)
        y_hi_col = jnp.where(y_high, vz[:, width - 1:width], y_hi_col)
        ym = jnp.where(lane == 0, y_lo_col, ym)
        yp = jnp.where(lane == width - 1, y_hi_col, yp)
        lap_z = zp + zm - 2.0 * vz
        lap_x = xp + xm - 2.0 * vz
        lap_y = yp + ym - 2.0 * vz
        react_v, new_w = cell_kinetics(vz, w_ref[z], into_voxel[z * rows_x:(z + 1) * rows_x])
        nv = vz + (cz_ref[z] * lap_z + cx_ref[z] * lap_x + cy_ref[z] * lap_y) + react_v
        nv_ref[z] = nv
        nw_ref[z] = new_w
        if not pack:
            continue
        xf_ref[z:z + 1, :] = nv[0:1, :]
        xl_ref[z:z + 1, :] = nv[rows_x - 1:rows_x, :]
        y_first[row_at] = y_first[row_at] + jnp.sum(
            jnp.where(pick, nv[:, 0:1], 0.0), axis=0, keepdims=True)
        y_last[row_at] = y_last[row_at] + jnp.sum(
            jnp.where(pick, nv[:, width - 1:width], 0.0), axis=0, keepdims=True)
    if not pack:
        return
    for i in range(face_rows):
        yf_ref[i:i + 1, :] = y_first[i]
        yl_ref[i:i + 1, :] = y_last[i]
    zs_ref[...] = jnp.where(z_low, nv_ref[depth - 1], nv_ref[0])

    snd_ref[:, 0:width] = one_hot_dot(oh_sblk_ref[...], nv_ref[...].reshape(depth * rows_x, width))
    snd_ref[:, width:2 * width] = one_hot_dot(oh_ids_t_ref[...], ntv_ref[...])


def coef_kernel(table_ref, cls_ref, cz_ref, cx_ref, cy_ref):
    for z in range(cls_ref.shape[0]):
        klass = cls_ref[z]
        outs = [jnp.zeros(klass.shape, jnp.float32) for _ in range(3)]
        for k in range(NCLASS):
            hit = klass == k
            outs = [jnp.where(hit, table_ref[d, k], outs[d]) for d in range(3)]
        cz_ref[z], cx_ref[z], cy_ref[z] = outs


def coefficients(fiber_class, fiber_table):
    shape = jax.ShapeDtypeStruct(fiber_class.shape, jnp.float32)
    vmem = pl.BlockSpec(memory_space=pltpu.VMEM)
    return pl.pallas_call(
        coef_kernel,
        out_shape=(shape, shape, shape),
        in_specs=[pl.BlockSpec(memory_space=pltpu.SMEM), vmem],
        out_specs=[vmem] * 3,
        interpret=INTERPRET,
    )(fiber_table, fiber_class)


def run_step(tables, state, recv, tile_gain, gains_rows, cable_rows, halos, pack):
    volt, recovery, coef_z, coef_x, coef_y, term_volt, term_recovery = state
    depth, rows_x, width = volt.shape
    slots = recv.shape[0]
    first = tile_gain is None
    f32 = jnp.float32
    smem = pl.BlockSpec(memory_space=pltpu.SMEM)
    vmem = pl.BlockSpec(memory_space=pltpu.VMEM)
    out_shape = (
        jax.ShapeDtypeStruct(volt.shape, f32),
        jax.ShapeDtypeStruct(volt.shape, f32),
        jax.ShapeDtypeStruct(term_volt.shape, f32),
        jax.ShapeDtypeStruct(term_volt.shape, f32),
    )
    if pack:
        out_shape += (
            jax.ShapeDtypeStruct((slots, 2 * width), f32),
            jax.ShapeDtypeStruct((rows_x, width), f32),
            jax.ShapeDtypeStruct((depth, width), f32),
            jax.ShapeDtypeStruct((depth, width), f32),
            jax.ShapeDtypeStruct((depth * rows_x // width, width), f32),
            jax.ShapeDtypeStruct((depth * rows_x // width, width), f32),
        )
    if first:
        out_shape += (jax.ShapeDtypeStruct((tables[1][2].shape[0], width), f32),)
    edges, one_hots = tables
    operands = ((edges, volt, recovery, coef_z, coef_x, coef_y, recv) + (() if first else (tile_gain,))
                + (gains_rows, term_volt, term_recovery, cable_rows) + tuple(halos) + tuple(one_hots))
    outs = pl.pallas_call(
        functools.partial(step_kernel, first=first, pack=pack),
        out_shape=out_shape,
        in_specs=[smem] + [vmem] * (len(operands) - 1),
        out_specs=[vmem] * len(out_shape),
        interpret=INTERPRET,
    )(*operands)
    return outs


def exchange_halos(faces):
    z_send, x_first, x_last, y_first, y_last = faces
    assert lax.axis_size("gz") == 2
    halos = [lax.ppermute(z_send, "gz", [(0, 1), (1, 0)])]
    for axis, first, last in (("gx", x_first, x_last), ("gy", y_first, y_last)):
        count = lax.axis_size(axis)
        halos.append(lax.ppermute(last, axis, [(i, i + 1) for i in range(count - 1)]))
        halos.append(lax.ppermute(first, axis, [(i + 1, i) for i in range(count - 1)]))
    return halos


def on_device(
    volt,
    recovery,
    fiber_class,
    fiber_table,
    junction_block,
    junction_term,
    junction_owner,
    term_volt,
    term_recovery,
    term_gain,
    cable_gain,
):
    depth, rows_x, width = volt.shape
    owners = lax.axis_size("gx") * lax.axis_size("gy")
    jcount = junction_block.shape[0]
    capacity = max(2, 2 * jcount // owners)
    slots_total = owners * capacity
    term_count = term_volt.shape[0]
    coef_z, coef_x, coef_y = coefficients(fiber_class, fiber_table)

    owner = junction_owner[:, 0]
    order = jnp.arange(jcount, dtype=jnp.int32)
    earlier = (owner[:, None] == owner[None, :]) & (order[None, :] < order[:, None])
    rank = jnp.sum(earlier.astype(jnp.int32), axis=1)
    slot = owner * capacity + rank
    hits = slot[None, :] == jnp.arange(slots_total, dtype=jnp.int32)[:, None]
    slot_block = jnp.sum(jnp.where(hits, junction_block[None, :], 0), axis=1)
    slot_term = jnp.sum(jnp.where(hits, junction_term[None, :] + 1, 0), axis=1) - 1

    arrived = lax.all_to_all(slot_term, ("gx", "gy"), split_axis=0, concat_axis=0, tiled=True)
    valid = arrived >= 0
    safe_ids = jnp.where(valid, arrived, 0)
    pick = safe_ids[:, None] == jnp.arange(term_count, dtype=jnp.int32)[None, :]
    gains = jnp.where(valid, jnp.sum(jnp.where(pick, term_gain[None, :], 0.0), axis=1), 0.0)
    gain_rows = jnp.broadcast_to(gains[:, None], (slots_total, width))
    cable_rows = jnp.broadcast_to(cable_gain[:, None], term_volt.shape)

    edges = []
    for axis in ("gz", "gx", "gy"):
        index = lax.axis_index(axis)
        edges += [index == 0, index == lax.axis_size(axis) - 1]
    edges = jnp.stack(edges + edges[:2]).astype(jnp.int32)
    bf16 = jnp.bfloat16
    rows_all = jnp.arange(depth * rows_x, dtype=jnp.int32)
    oh_blk = (junction_block[:, None] == rows_all[None, :]).astype(bf16)
    oh_slot = (slot[:, None] == jnp.arange(slots_total, dtype=jnp.int32)[None, :]).astype(bf16)
    oh_ids = (jnp.arange(term_count, dtype=jnp.int32)[:, None] == safe_ids[None, :]).astype(bf16)
    oh_sblk = (slot_block[:, None] == rows_all[None, :]).astype(bf16)
    one_hots = (oh_blk, oh_blk.T, oh_slot, oh_ids, oh_ids.T, oh_sblk)
    tables = (edges, one_hots)

    flat_rows = volt.reshape(depth * rows_x, width)
    sent = jnp.concatenate([flat_rows[slot_block], term_volt[safe_ids], gain_rows], axis=1)
    faces = (
        jnp.where(lax.axis_index("gz") == 0, volt[depth - 1], volt[0]),
        volt[:, 0, :],
        volt[:, rows_x - 1, :],
        volt[:, :, 0].reshape(-1, width),
        volt[:, :, width - 1].reshape(-1, width),
    )
    faces, sent = lax.optimization_barrier((faces, sent))
    tile_gain = None
    for step in range(STEPS):
        halos = exchange_halos(faces)
        received = lax.all_to_all(sent, ("gx", "gy"), split_axis=0, concat_axis=0, tiled=True)
        state = (volt, recovery, coef_z, coef_x, coef_y, term_volt, term_recovery)
        pack = step < STEPS - 1
        outs = run_step(tables, state, received, tile_gain, gain_rows, cable_rows, halos, pack)
        if step == 0:
            tile_gain = outs[-1]
        volt, recovery, term_volt, term_recovery = outs[:4]
        if pack:
            sent, faces = outs[4], outs[5:10]
    return (volt, recovery, term_volt, term_recovery)


def solution(mesh):
    return jax.shard_map(
        on_device,
        mesh=mesh,
        in_specs=(
            P("gz", "gx", "gy"),
            P("gz", "gx", "gy"),
            P("gz", "gx", "gy"),
            P(),
            P(("gx", "gy", "gz")),
            P(("gx", "gy", "gz")),
            P(("gx", "gy", "gz"), None),
            P(("gx", "gy", "gz"), None),
            P(("gx", "gy", "gz"), None),
            P(("gx", "gy", "gz")),
            P(("gx", "gy", "gz")),
        ),
        out_specs=(
            P("gz", "gx", "gy"),
            P("gz", "gx", "gy"),
            P(("gx", "gy", "gz"), None),
            P(("gx", "gy", "gz"), None),
        ),
        check_vma=False,
    )
```

```python
import functools

import jax
import jax.numpy as jnp
from jax import lax
from jax.experimental import pallas as pl
from jax.experimental.pallas import tpu as pltpu
from jax.sharding import PartitionSpec as P

NCLASS = 8
STEPS = 4
INTERPRET = False


def cell_kinetics(v, w, drive):
    react = -8.0 * v * (v - 0.15) * (v - 1.0) - v * w
    new_v = 0.1 * (react + drive)
    new_w = w + 0.01 * (-w - 8.0 * v * (v - 1.15))
    return (new_v, new_w)


def shifted(cells, axis):
    size = cells.shape[axis]
    a = pltpu.roll(cells, 1, axis)
    b = pltpu.roll(cells, size - 1, axis)
    pos = lax.broadcasted_iota(jnp.int32, cells.shape, axis)
    moved = pltpu.roll(pos, 1, axis)
    forward = moved == jnp.where(pos == 0, size - 1, pos - 1)
    return jnp.where(forward, a, b), jnp.where(forward, b, a)


def flag(ref, i, shape):
    return jnp.full(shape, ref[i], jnp.int32) > 0


def split3(x):
    a = x.astype(jnp.bfloat16)
    rest = x - a.astype(jnp.float32)
    b = rest.astype(jnp.bfloat16)
    c = (rest - b.astype(jnp.float32)).astype(jnp.bfloat16)
    return a, b, c


def one_hot_dot(one_hot, x):
    a, b, c = split3(x)
    if INTERPRET:
        one_hot, a, b, c = (t.astype(jnp.float32) for t in (one_hot, a, b, c))
    dot = lambda part: jnp.dot(one_hot, part, preferred_element_type=jnp.float32)
    return (dot(a) + dot(b)) + dot(c)


def step_kernel(*refs, first, pack):
    refs = iter(refs)
    edge_ref, v_ref, w_ref, cz_ref, cx_ref, cy_ref, recv_ref = (next(refs) for _ in range(7))
    tg_ref = None if first else next(refs)
    g_ref, tv_ref, tr_ref, cg_ref, zr_ref, xlo_ref, xhi_ref, ylo_ref, yhi_ref = (next(refs) for _ in range(9))
    oh_blk_ref, oh_blk_t_ref, oh_slot_ref, oh_ids_ref, oh_ids_t_ref, oh_sblk_ref = (next(refs) for _ in range(6))
    nv_ref, nw_ref, ntv_ref, ntr_ref = (next(refs) for _ in range(4))
    if pack:
        snd_ref, zs_ref, xf_ref, xl_ref, yf_ref, yl_ref = (next(refs) for _ in range(6))
    depth, rows_x, width = v_ref.shape
    if first:
        tile_gain = one_hot_dot(oh_slot_ref[...], recv_ref[:, 2 * width:3 * width])
        next(refs)[...] = tile_gain
    else:
        tile_gain = tg_ref[...]

    v_flat = v_ref[...].reshape(depth * rows_x, width)
    rows = one_hot_dot(oh_blk_ref[...], v_flat)
    far = one_hot_dot(oh_slot_ref[...], recv_ref[:, width:2 * width])
    tile_current = tile_gain * (far - rows)
    into_voxel = one_hot_dot(oh_blk_t_ref[...], tile_current)

    far_volt = one_hot_dot(oh_ids_t_ref[...], tv_ref[...])
    current = g_ref[...] * (far_volt - recv_ref[:, 0:width])
    into_term = one_hot_dot(oh_ids_ref[...], -current)

    u = tv_ref[...]
    r = tr_ref[...]
    u_minus, u_plus = shifted(u, 1)
    lane_t = lax.broadcasted_iota(jnp.int32, u.shape, 1)
    u_minus = jnp.where(lane_t == 0, u, u_minus)
    u_plus = jnp.where(lane_t == width - 1, u, u_plus)
    lap_k = u_plus + u_minus - 2.0 * u
    react_u, new_r = cell_kinetics(u, r, 0.1 * into_term)
    ntv_ref[...] = u + cg_ref[...] * lap_k + react_u
    ntr_ref[...] = new_r

    plane = (rows_x, width)
    sub = lax.broadcasted_iota(jnp.int32, plane, 0)
    lane = lax.broadcasted_iota(jnp.int32, plane, 1)
    z_low = flag(edge_ref, 0, plane)
    z_high = flag(edge_ref, 1, plane)
    x_low = flag(edge_ref, 2, (1, width))
    x_high = flag(edge_ref, 3, (1, width))
    y_low = flag(edge_ref, 4, (rows_x, 1))
    y_high = flag(edge_ref, 5, (rows_x, 1))
    per_row = width // rows_x
    face_rows = depth * rows_x // width
    y_first = [jnp.zeros((1, width), jnp.float32) for _ in range(face_rows)]
    y_last = [jnp.zeros((1, width), jnp.float32) for _ in range(face_rows)]
    for z in range(depth):
        vz = v_ref[z]
        if z == 0:
            zm = jnp.where(z_low, vz, zr_ref[...])
        else:
            zm = v_ref[z - 1]
        if z == depth - 1:
            zp = jnp.where(z_high, vz, zr_ref[...])
        else:
            zp = v_ref[z + 1]
        xm, xp = shifted(vz, 0)
        x_lo_row = jnp.where(x_low, vz[0:1, :], xlo_ref[z:z + 1, :])
        x_hi_row = jnp.where(x_high, vz[rows_x - 1:rows_x, :], xhi_ref[z:z + 1, :])
        xm = jnp.where(sub == 0, x_lo_row, xm)
        xp = jnp.where(sub == rows_x - 1, x_hi_row, xp)
        ym, yp = shifted(vz, 1)
        row_at, lane_at = z // per_row, (z % per_row) * rows_x
        pick = lane == sub + lane_at
        y_lo_col = jnp.sum(jnp.where(pick, ylo_ref[row_at:row_at + 1, :], 0.0), axis=1, keepdims=True)
        y_hi_col = jnp.sum(jnp.where(pick, yhi_ref[row_at:row_at + 1, :], 0.0), axis=1, keepdims=True)
        y_lo_col = jnp.where(y_low, vz[:, 0:1], y_lo_col)
        y_hi_col = jnp.where(y_high, vz[:, width - 1:width], y_hi_col)
        ym = jnp.where(lane == 0, y_lo_col, ym)
        yp = jnp.where(lane == width - 1, y_hi_col, yp)
        lap_z = zp + zm - 2.0 * vz
        lap_x = xp + xm - 2.0 * vz
        lap_y = yp + ym - 2.0 * vz
        react_v, new_w = cell_kinetics(vz, w_ref[z], into_voxel[z * rows_x:(z + 1) * rows_x])
        nv = vz + (cz_ref[z] * lap_z + cx_ref[z] * lap_x + cy_ref[z] * lap_y) + react_v
        nv_ref[z] = nv
        nw_ref[z] = new_w
        if not pack:
            continue
        xf_ref[z:z + 1, :] = nv[0:1, :]
        xl_ref[z:z + 1, :] = nv[rows_x - 1:rows_x, :]
        y_first[row_at] = y_first[row_at] + jnp.sum(
            jnp.where(pick, nv[:, 0:1], 0.0), axis=0, keepdims=True)
        y_last[row_at] = y_last[row_at] + jnp.sum(
            jnp.where(pick, nv[:, width - 1:width], 0.0), axis=0, keepdims=True)
    if not pack:
        return
    for i in range(face_rows):
        yf_ref[i:i + 1, :] = y_first[i]
        yl_ref[i:i + 1, :] = y_last[i]
    zs_ref[...] = jnp.where(z_low, nv_ref[depth - 1], nv_ref[0])

    dests, capacity = snd_ref.shape[0], snd_ref.shape[1]
    sel_rows = one_hot_dot(oh_sblk_ref[...], nv_ref[...].reshape(depth * rows_x, width))
    sel_volt = one_hot_dot(oh_ids_t_ref[...], ntv_ref[...])
    snd_ref[...] = jnp.concatenate([sel_rows, sel_volt], axis=1).reshape(dests, capacity, 2 * width)


def coef_kernel(table_ref, cls_ref, cz_ref, cx_ref, cy_ref):
    for z in range(cls_ref.shape[0]):
        klass = cls_ref[z]
        outs = [jnp.zeros(klass.shape, jnp.float32) for _ in range(3)]
        for k in range(NCLASS):
            hit = klass == k
            outs = [jnp.where(hit, table_ref[d, k], outs[d]) for d in range(3)]
        cz_ref[z], cx_ref[z], cy_ref[z] = outs


def coefficients(fiber_class, fiber_table):
    shape = jax.ShapeDtypeStruct(fiber_class.shape, jnp.float32)
    vmem = pl.BlockSpec(memory_space=pltpu.VMEM)
    return pl.pallas_call(
        coef_kernel,
        out_shape=(shape, shape, shape),
        in_specs=[pl.BlockSpec(memory_space=pltpu.SMEM), vmem],
        out_specs=[vmem] * 3,
        interpret=INTERPRET,
    )(fiber_table, fiber_class)


def run_step(tables, state, recv, tile_gain, gains_rows, cable_rows, halos, pack):
    volt, recovery, coef_z, coef_x, coef_y, term_volt, term_recovery = state
    depth, rows_x, width = volt.shape
    slots = recv.shape[0]
    first = tile_gain is None
    f32 = jnp.float32
    smem = pl.BlockSpec(memory_space=pltpu.SMEM)
    vmem = pl.BlockSpec(memory_space=pltpu.VMEM)
    out_shape = (
        jax.ShapeDtypeStruct(volt.shape, f32),
        jax.ShapeDtypeStruct(volt.shape, f32),
        jax.ShapeDtypeStruct(term_volt.shape, f32),
        jax.ShapeDtypeStruct(term_volt.shape, f32),
    )
    if pack:
        out_shape += (
            jax.ShapeDtypeStruct((slots // 2, 2, 2 * width), f32),
            jax.ShapeDtypeStruct((rows_x, width), f32),
            jax.ShapeDtypeStruct((depth, width), f32),
            jax.ShapeDtypeStruct((depth, width), f32),
            jax.ShapeDtypeStruct((depth * rows_x // width, width), f32),
            jax.ShapeDtypeStruct((depth * rows_x // width, width), f32),
        )
    if first:
        out_shape += (jax.ShapeDtypeStruct((tables[1][2].shape[0], width), f32),)
    edges, one_hots = tables
    operands = ((edges, volt, recovery, coef_z, coef_x, coef_y, recv) + (() if first else (tile_gain,))
                + (gains_rows, term_volt, term_recovery, cable_rows) + tuple(halos) + tuple(one_hots))
    outs = pl.pallas_call(
        functools.partial(step_kernel, first=first, pack=pack),
        out_shape=out_shape,
        in_specs=[smem] + [vmem] * (len(operands) - 1),
        out_specs=[vmem] * len(out_shape),
        interpret=INTERPRET,
    )(*operands)
    return outs


def exchange_halos(faces):
    z_send, x_first, x_last, y_first, y_last = faces
    assert lax.axis_size("gz") == 2
    halos = [lax.ppermute(z_send, "gz", [(0, 1), (1, 0)])]
    for axis, first, last in (("gx", x_first, x_last), ("gy", y_first, y_last)):
        count = lax.axis_size(axis)
        halos.append(lax.ppermute(last, axis, [(i, i + 1) for i in range(count - 1)]))
        halos.append(lax.ppermute(first, axis, [(i + 1, i) for i in range(count - 1)]))
    return halos


def on_device(
    volt,
    recovery,
    fiber_class,
    fiber_table,
    junction_block,
    junction_term,
    junction_owner,
    term_volt,
    term_recovery,
    term_gain,
    cable_gain,
):
    depth, rows_x, width = volt.shape
    owners = lax.axis_size("gx") * lax.axis_size("gy")
    jcount = junction_block.shape[0]
    capacity = max(2, 2 * jcount // owners)
    slots_total = owners * capacity
    term_count = term_volt.shape[0]
    coef_z, coef_x, coef_y = coefficients(fiber_class, fiber_table)

    owner = junction_owner[:, 0]
    order = jnp.arange(jcount, dtype=jnp.int32)
    earlier = (owner[:, None] == owner[None, :]) & (order[None, :] < order[:, None])
    rank = jnp.sum(earlier.astype(jnp.int32), axis=1)
    slot = owner * capacity + rank
    hits = slot[None, :] == jnp.arange(slots_total, dtype=jnp.int32)[:, None]
    slot_block = jnp.sum(jnp.where(hits, junction_block[None, :], 0), axis=1)
    slot_term = jnp.sum(jnp.where(hits, junction_term[None, :] + 1, 0), axis=1) - 1

    arrived = lax.all_to_all(slot_term, ("gx", "gy"), split_axis=0, concat_axis=0, tiled=True)
    valid = arrived >= 0
    safe_ids = jnp.where(valid, arrived, 0)
    pick = safe_ids[:, None] == jnp.arange(term_count, dtype=jnp.int32)[None, :]
    gains = jnp.where(valid, jnp.sum(jnp.where(pick, term_gain[None, :], 0.0), axis=1), 0.0)
    gain_rows = jnp.broadcast_to(gains[:, None], (slots_total, width))
    cable_rows = jnp.broadcast_to(cable_gain[:, None], term_volt.shape)

    edges = []
    for axis in ("gz", "gx", "gy"):
        index = lax.axis_index(axis)
        edges += [index == 0, index == lax.axis_size(axis) - 1]
    edges = jnp.stack(edges + edges[:2]).astype(jnp.int32)
    bf16 = jnp.bfloat16
    rows_all = jnp.arange(depth * rows_x, dtype=jnp.int32)
    oh_blk = (junction_block[:, None] == rows_all[None, :]).astype(bf16)
    oh_slot = (slot[:, None] == jnp.arange(slots_total, dtype=jnp.int32)[None, :]).astype(bf16)
    oh_ids = (jnp.arange(term_count, dtype=jnp.int32)[:, None] == safe_ids[None, :]).astype(bf16)
    oh_sblk = (slot_block[:, None] == rows_all[None, :]).astype(bf16)
    one_hots = (oh_blk, oh_blk.T, oh_slot, oh_ids, oh_ids.T, oh_sblk)
    tables = (edges, one_hots)

    flat_rows = volt.reshape(depth * rows_x, width)
    sent = jnp.concatenate([flat_rows[slot_block], term_volt[safe_ids], gain_rows], axis=1)
    faces = (
        jnp.where(lax.axis_index("gz") == 0, volt[depth - 1], volt[0]),
        volt[:, 0, :],
        volt[:, rows_x - 1, :],
        volt[:, :, 0].reshape(-1, width),
        volt[:, :, width - 1].reshape(-1, width),
    )
    faces, sent = lax.optimization_barrier((faces, sent))
    tile_gain = None
    for step in range(STEPS):
        halos = exchange_halos(faces)
        received = lax.all_to_all(sent, ("gx", "gy"), split_axis=0, concat_axis=0, tiled=True)
        state = (volt, recovery, coef_z, coef_x, coef_y, term_volt, term_recovery)
        pack = step < STEPS - 1
        outs = run_step(tables, state, received, tile_gain, gain_rows, cable_rows, halos, pack)
        if step == 0:
            tile_gain = outs[-1]
        volt, recovery, term_volt, term_recovery = outs[:4]
        if pack:
            sent, faces = outs[4].reshape(slots_total, 2 * width), outs[5:10]
    return (volt, recovery, term_volt, term_recovery)


def solution(mesh):
    return jax.shard_map(
        on_device,
        mesh=mesh,
        in_specs=(
            P("gz", "gx", "gy"),
            P("gz", "gx", "gy"),
            P("gz", "gx", "gy"),
            P(),
            P(("gx", "gy", "gz")),
            P(("gx", "gy", "gz")),
            P(("gx", "gy", "gz"), None),
            P(("gx", "gy", "gz"), None),
            P(("gx", "gy", "gz"), None),
            P(("gx", "gy", "gz")),
            P(("gx", "gy", "gz")),
        ),
        out_specs=(
            P("gz", "gx", "gy"),
            P("gz", "gx", "gy"),
            P(("gx", "gy", "gz"), None),
            P(("gx", "gy", "gz"), None),
        ),
        check_vma=False,
    )
```

```python
import functools

import jax
import jax.numpy as jnp
from jax import lax
from jax.experimental import pallas as pl
from jax.experimental.pallas import tpu as pltpu
from jax.sharding import PartitionSpec as P

NCLASS = 8
STEPS = 4
INTERPRET = False


def cell_kinetics(v, w, drive):
    react = -8.0 * v * (v - 0.15) * (v - 1.0) - v * w
    new_v = 0.1 * (react + drive)
    new_w = w + 0.01 * (-w - 8.0 * v * (v - 1.15))
    return (new_v, new_w)


def shifted(cells, axis):
    size = cells.shape[axis]
    a = pltpu.roll(cells, 1, axis)
    b = pltpu.roll(cells, size - 1, axis)
    pos = lax.broadcasted_iota(jnp.int32, cells.shape, axis)
    moved = pltpu.roll(pos, 1, axis)
    forward = moved == jnp.where(pos == 0, size - 1, pos - 1)
    return jnp.where(forward, a, b), jnp.where(forward, b, a)


def flag(ref, i, shape):
    return jnp.full(shape, ref[i], jnp.int32) > 0


def split3(x):
    a = x.astype(jnp.bfloat16)
    rest = x - a.astype(jnp.float32)
    b = rest.astype(jnp.bfloat16)
    c = (rest - b.astype(jnp.float32)).astype(jnp.bfloat16)
    return a, b, c


def one_hot_dot(one_hot, x):
    a, b, c = split3(x)
    if INTERPRET:
        one_hot, a, b, c = (t.astype(jnp.float32) for t in (one_hot, a, b, c))
    dot = lambda part: jnp.dot(one_hot, part, preferred_element_type=jnp.float32)
    return (dot(a) + dot(b)) + dot(c)


def step_kernel(*refs, first, pack):
    refs = iter(refs)
    edge_ref, v_ref, w_ref, cz_ref, cx_ref, cy_ref, recv_ref = (next(refs) for _ in range(7))
    tg_ref = None if first else next(refs)
    g_ref, tv_ref, tr_ref, cg_ref, zr_ref, xlo_ref, xhi_ref, ylo_ref, yhi_ref = (next(refs) for _ in range(9))
    oh_blk_ref, oh_blk_t_ref, oh_slot_ref, oh_ids_ref, oh_ids_t_ref, oh_sblk_ref = (next(refs) for _ in range(6))
    nv_ref, nw_ref, ntv_ref, ntr_ref = (next(refs) for _ in range(4))
    if pack:
        snd_ref, zs_ref, xf_ref, xl_ref, yf_ref, yl_ref = (next(refs) for _ in range(6))
    depth, rows_x, width = v_ref.shape
    recv = recv_ref[...]
    recv = recv.reshape(recv.shape[0] * recv.shape[1], recv.shape[2])
    if first:
        tile_gain = one_hot_dot(oh_slot_ref[...], recv[:, 2 * width:3 * width])
        next(refs)[...] = tile_gain
    else:
        tile_gain = tg_ref[...]

    v_flat = v_ref[...].reshape(depth * rows_x, width)
    rows = one_hot_dot(oh_blk_ref[...], v_flat)
    far = one_hot_dot(oh_slot_ref[...], recv[:, width:2 * width])
    tile_current = tile_gain * (far - rows)
    into_voxel = one_hot_dot(oh_blk_t_ref[...], tile_current)

    far_volt = one_hot_dot(oh_ids_t_ref[...], tv_ref[...])
    current = g_ref[...] * (far_volt - recv[:, 0:width])
    into_term = one_hot_dot(oh_ids_ref[...], -current)

    u = tv_ref[...]
    r = tr_ref[...]
    u_minus, u_plus = shifted(u, 1)
    lane_t = lax.broadcasted_iota(jnp.int32, u.shape, 1)
    u_minus = jnp.where(lane_t == 0, u, u_minus)
    u_plus = jnp.where(lane_t == width - 1, u, u_plus)
    lap_k = u_plus + u_minus - 2.0 * u
    react_u, new_r = cell_kinetics(u, r, 0.1 * into_term)
    ntv_ref[...] = u + cg_ref[...] * lap_k + react_u
    ntr_ref[...] = new_r

    plane = (rows_x, width)
    sub = lax.broadcasted_iota(jnp.int32, plane, 0)
    lane = lax.broadcasted_iota(jnp.int32, plane, 1)
    z_low = flag(edge_ref, 0, plane)
    z_high = flag(edge_ref, 1, plane)
    x_low = flag(edge_ref, 2, (1, width))
    x_high = flag(edge_ref, 3, (1, width))
    y_low = flag(edge_ref, 4, (rows_x, 1))
    y_high = flag(edge_ref, 5, (rows_x, 1))
    per_row = width // rows_x
    face_rows = depth * rows_x // width
    y_first = [jnp.zeros((1, width), jnp.float32) for _ in range(face_rows)]
    y_last = [jnp.zeros((1, width), jnp.float32) for _ in range(face_rows)]
    for z in range(depth):
        vz = v_ref[z]
        if z == 0:
            zm = jnp.where(z_low, vz, zr_ref[...])
        else:
            zm = v_ref[z - 1]
        if z == depth - 1:
            zp = jnp.where(z_high, vz, zr_ref[...])
        else:
            zp = v_ref[z + 1]
        xm, xp = shifted(vz, 0)
        x_lo_row = jnp.where(x_low, vz[0:1, :], xlo_ref[z:z + 1, :])
        x_hi_row = jnp.where(x_high, vz[rows_x - 1:rows_x, :], xhi_ref[z:z + 1, :])
        xm = jnp.where(sub == 0, x_lo_row, xm)
        xp = jnp.where(sub == rows_x - 1, x_hi_row, xp)
        ym, yp = shifted(vz, 1)
        row_at, lane_at = z // per_row, (z % per_row) * rows_x
        pick = lane == sub + lane_at
        y_lo_col = jnp.sum(jnp.where(pick, ylo_ref[row_at:row_at + 1, :], 0.0), axis=1, keepdims=True)
        y_hi_col = jnp.sum(jnp.where(pick, yhi_ref[row_at:row_at + 1, :], 0.0), axis=1, keepdims=True)
        y_lo_col = jnp.where(y_low, vz[:, 0:1], y_lo_col)
        y_hi_col = jnp.where(y_high, vz[:, width - 1:width], y_hi_col)
        ym = jnp.where(lane == 0, y_lo_col, ym)
        yp = jnp.where(lane == width - 1, y_hi_col, yp)
        lap_z = zp + zm - 2.0 * vz
        lap_x = xp + xm - 2.0 * vz
        lap_y = yp + ym - 2.0 * vz
        react_v, new_w = cell_kinetics(vz, w_ref[z], into_voxel[z * rows_x:(z + 1) * rows_x])
        nv = vz + (cz_ref[z] * lap_z + cx_ref[z] * lap_x + cy_ref[z] * lap_y) + react_v
        nv_ref[z] = nv
        nw_ref[z] = new_w
        if not pack:
            continue
        xf_ref[z:z + 1, :] = nv[0:1, :]
        xl_ref[z:z + 1, :] = nv[rows_x - 1:rows_x, :]
        y_first[row_at] = y_first[row_at] + jnp.sum(
            jnp.where(pick, nv[:, 0:1], 0.0), axis=0, keepdims=True)
        y_last[row_at] = y_last[row_at] + jnp.sum(
            jnp.where(pick, nv[:, width - 1:width], 0.0), axis=0, keepdims=True)
    if not pack:
        return
    for i in range(face_rows):
        yf_ref[i:i + 1, :] = y_first[i]
        yl_ref[i:i + 1, :] = y_last[i]
    zs_ref[...] = jnp.where(z_low, nv_ref[depth - 1], nv_ref[0])

    dests, capacity = snd_ref.shape[0], snd_ref.shape[1]
    sel_rows = one_hot_dot(oh_sblk_ref[...], nv_ref[...].reshape(depth * rows_x, width))
    sel_volt = one_hot_dot(oh_ids_t_ref[...], ntv_ref[...])
    snd_ref[...] = jnp.concatenate([sel_rows, sel_volt], axis=1).reshape(dests, capacity, 2 * width)


def coef_kernel(table_ref, cls_ref, cz_ref, cx_ref, cy_ref):
    for z in range(cls_ref.shape[0]):
        klass = cls_ref[z]
        outs = [jnp.zeros(klass.shape, jnp.float32) for _ in range(3)]
        for k in range(NCLASS):
            hit = klass == k
            outs = [jnp.where(hit, table_ref[d, k], outs[d]) for d in range(3)]
        cz_ref[z], cx_ref[z], cy_ref[z] = outs


def coefficients(fiber_class, fiber_table):
    shape = jax.ShapeDtypeStruct(fiber_class.shape, jnp.float32)
    vmem = pl.BlockSpec(memory_space=pltpu.VMEM)
    return pl.pallas_call(
        coef_kernel,
        out_shape=(shape, shape, shape),
        in_specs=[pl.BlockSpec(memory_space=pltpu.SMEM), vmem],
        out_specs=[vmem] * 3,
        interpret=INTERPRET,
    )(fiber_table, fiber_class)


def run_step(tables, state, recv, tile_gain, gains_rows, cable_rows, halos, pack):
    volt, recovery, coef_z, coef_x, coef_y, term_volt, term_recovery = state
    depth, rows_x, width = volt.shape
    slots = recv.shape[0] * recv.shape[1]
    first = tile_gain is None
    f32 = jnp.float32
    smem = pl.BlockSpec(memory_space=pltpu.SMEM)
    vmem = pl.BlockSpec(memory_space=pltpu.VMEM)
    out_shape = (
        jax.ShapeDtypeStruct(volt.shape, f32),
        jax.ShapeDtypeStruct(volt.shape, f32),
        jax.ShapeDtypeStruct(term_volt.shape, f32),
        jax.ShapeDtypeStruct(term_volt.shape, f32),
    )
    if pack:
        out_shape += (
            jax.ShapeDtypeStruct((slots // 2, 2, 2 * width), f32),
            jax.ShapeDtypeStruct((rows_x, width), f32),
            jax.ShapeDtypeStruct((depth, width), f32),
            jax.ShapeDtypeStruct((depth, width), f32),
            jax.ShapeDtypeStruct((depth * rows_x // width, width), f32),
            jax.ShapeDtypeStruct((depth * rows_x // width, width), f32),
        )
    if first:
        out_shape += (jax.ShapeDtypeStruct((tables[1][2].shape[0], width), f32),)
    edges, one_hots = tables
    operands = ((edges, volt, recovery, coef_z, coef_x, coef_y, recv) + (() if first else (tile_gain,))
                + (gains_rows, term_volt, term_recovery, cable_rows) + tuple(halos) + tuple(one_hots))
    outs = pl.pallas_call(
        functools.partial(step_kernel, first=first, pack=pack),
        out_shape=out_shape,
        in_specs=[smem] + [vmem] * (len(operands) - 1),
        out_specs=[vmem] * len(out_shape),
        interpret=INTERPRET,
    )(*operands)
    return outs


def exchange_halos(faces):
    z_send, x_first, x_last, y_first, y_last = faces
    assert lax.axis_size("gz") == 2
    halos = [lax.ppermute(z_send, "gz", [(0, 1), (1, 0)])]
    for axis, first, last in (("gx", x_first, x_last), ("gy", y_first, y_last)):
        count = lax.axis_size(axis)
        halos.append(lax.ppermute(last, axis, [(i, i + 1) for i in range(count - 1)]))
        halos.append(lax.ppermute(first, axis, [(i + 1, i) for i in range(count - 1)]))
    return halos


def on_device(
    volt,
    recovery,
    fiber_class,
    fiber_table,
    junction_block,
    junction_term,
    junction_owner,
    term_volt,
    term_recovery,
    term_gain,
    cable_gain,
):
    depth, rows_x, width = volt.shape
    owners = lax.axis_size("gx") * lax.axis_size("gy")
    jcount = junction_block.shape[0]
    capacity = max(2, 2 * jcount // owners)
    slots_total = owners * capacity
    term_count = term_volt.shape[0]
    coef_z, coef_x, coef_y = coefficients(fiber_class, fiber_table)

    owner = junction_owner[:, 0]
    order = jnp.arange(jcount, dtype=jnp.int32)
    earlier = (owner[:, None] == owner[None, :]) & (order[None, :] < order[:, None])
    rank = jnp.sum(earlier.astype(jnp.int32), axis=1)
    slot = owner * capacity + rank
    hits = slot[None, :] == jnp.arange(slots_total, dtype=jnp.int32)[:, None]
    slot_block = jnp.sum(jnp.where(hits, junction_block[None, :], 0), axis=1)
    slot_term = jnp.sum(jnp.where(hits, junction_term[None, :] + 1, 0), axis=1) - 1

    arrived = lax.all_to_all(slot_term, ("gx", "gy"), split_axis=0, concat_axis=0, tiled=True)
    valid = arrived >= 0
    safe_ids = jnp.where(valid, arrived, 0)
    pick = safe_ids[:, None] == jnp.arange(term_count, dtype=jnp.int32)[None, :]
    gains = jnp.where(valid, jnp.sum(jnp.where(pick, term_gain[None, :], 0.0), axis=1), 0.0)
    gain_rows = jnp.broadcast_to(gains[:, None], (slots_total, width))
    cable_rows = jnp.broadcast_to(cable_gain[:, None], term_volt.shape)

    edges = []
    for axis in ("gz", "gx", "gy"):
        index = lax.axis_index(axis)
        edges += [index == 0, index == lax.axis_size(axis) - 1]
    edges = jnp.stack(edges + edges[:2]).astype(jnp.int32)
    bf16 = jnp.bfloat16
    rows_all = jnp.arange(depth * rows_x, dtype=jnp.int32)
    oh_blk = (junction_block[:, None] == rows_all[None, :]).astype(bf16)
    oh_slot = (slot[:, None] == jnp.arange(slots_total, dtype=jnp.int32)[None, :]).astype(bf16)
    oh_ids = (jnp.arange(term_count, dtype=jnp.int32)[:, None] == safe_ids[None, :]).astype(bf16)
    oh_sblk = (slot_block[:, None] == rows_all[None, :]).astype(bf16)
    one_hots = (oh_blk, oh_blk.T, oh_slot, oh_ids, oh_ids.T, oh_sblk)
    tables = (edges, one_hots)

    flat_rows = volt.reshape(depth * rows_x, width)
    sent = jnp.concatenate([flat_rows[slot_block], term_volt[safe_ids], gain_rows], axis=1)
    faces = (
        jnp.where(lax.axis_index("gz") == 0, volt[depth - 1], volt[0]),
        volt[:, 0, :],
        volt[:, rows_x - 1, :],
        volt[:, :, 0].reshape(-1, width),
        volt[:, :, width - 1].reshape(-1, width),
    )
    faces, sent = lax.optimization_barrier((faces, sent))
    tile_gain = None
    for step in range(STEPS):
        halos = exchange_halos(faces)
        sent = sent.reshape(owners, capacity, sent.shape[-1])
        received = lax.all_to_all(sent, ("gx", "gy"), split_axis=0, concat_axis=0, tiled=True)
        state = (volt, recovery, coef_z, coef_x, coef_y, term_volt, term_recovery)
        pack = step < STEPS - 1
        outs = run_step(tables, state, received, tile_gain, gain_rows, cable_rows, halos, pack)
        if step == 0:
            tile_gain = outs[-1]
        volt, recovery, term_volt, term_recovery = outs[:4]
        if pack:
            sent, faces = outs[4], outs[5:10]
    return (volt, recovery, term_volt, term_recovery)


def solution(mesh):
    return jax.shard_map(
        on_device,
        mesh=mesh,
        in_specs=(
            P("gz", "gx", "gy"),
            P("gz", "gx", "gy"),
            P("gz", "gx", "gy"),
            P(),
            P(("gx", "gy", "gz")),
            P(("gx", "gy", "gz")),
            P(("gx", "gy", "gz"), None),
            P(("gx", "gy", "gz"), None),
            P(("gx", "gy", "gz"), None),
            P(("gx", "gy", "gz")),
            P(("gx", "gy", "gz")),
        ),
        out_specs=(
            P("gz", "gx", "gy"),
            P("gz", "gx", "gy"),
            P(("gx", "gy", "gz"), None),
            P(("gx", "gy", "gz"), None),
        ),
        check_vma=False,
    )
```
